256 devices in a mesh: dp: 8 (over x, z_hi), ctx: 32 (over z_lo, y, core).
Axes of the slice: x: 4, y: 4, z: 8 (z_hi: 2, z_lo: 4; z = z_hi * 4 + z_lo), core: 2. Of those that a mesh axis runs over, the one named last changes fastest.
Arguments:
- queries: bfloat16 [32768, 1024], P(('dp', 'ctx')), parts along dimension 0, may hold values from -8 to 8
- keys: bfloat16 [32768, 1024], P(('dp', 'ctx')), parts along dimension 0, may hold values from -8 to 8
- values: bfloat16 [32768, 1024], P(('dp', 'ctx')), parts along dimension 0, may hold values from -6 to 6
- grad_out: bfloat16 [32768, 1024], P(('dp', 'ctx')), parts along dimension 0, may hold values from -6 to 6
- rand_blocks: int32 [512, 3], P(('dp', 'ctx')), parts along dimension 0, may hold values from 0 to 1
- global_ids: int32 [16], P('dp'), parts along dimension 0, may hold values from 0 to 63
Outputs:
- attended: bfloat16 [32768, 1024], P(('dp', 'ctx')), parts along dimension 0
- grad_queries: bfloat16 [32768, 1024], P(('dp', 'ctx')), parts along dimension 0
- grad_keys: bfloat16 [32768, 1024], P(('dp', 'ctx')), parts along dimension 0
- grad_values: bfloat16 [32768, 1024], P(('dp', 'ctx')), parts along dimension 0
The draws below stay inside these ranges and needn't reach their ends.
There are 8 independent parts, one for each index of `dp`. The reference program is written for one: setup_inputs(seed, part) draws one part's arguments, and reference() takes and returns one part's arrays. A program takes and returns all parts, laid end to end along the dimension named above; each array names one. Nothing has to cross between parts.
All inputs are finite; a program needn't handle non-finite values.
Results may differ from the reference program's by a relative error of at most 0.02.
Values may be sent and summed in bfloat16 or wider, within the bound.
No kernel may reach another device: no remote copies, remote signals or barrier semaphores. Data moves between devices by JAX's collectives and lax.ppermute only.
A program may use at most 128 MiB of HBM per device.

```python
import jax
import jax.numpy as jnp
from jax import lax

HEADS = 16
HEAD_DIM = 64
BLOCK = 64
RAND = 3
GLOBALS = 2
TOK_DEV = 128
D = 1024
SEQ = 4096
BLOCKS_DEV = 2
SEQ_BLOCKS = 64
N_CTX = 32


def paired_draw(key):
    first = jax.random.fold_in(key, 101)
    second = jax.random.fold_in(key, 202)
    query_field = jnp.clip(jax.random.normal(first, (SEQ, D), jnp.float32), -4.0, 4.0)
    key_field = jnp.clip(jax.random.normal(second, (SEQ, D), jnp.float32), -4.0, 4.0)
    return (query_field, key_field)


def draw_queries(key, part):
    return paired_draw(key)[0].astype(jnp.bfloat16)


def draw_keys(key, part):
    return paired_draw(key)[1].astype(jnp.bfloat16)


def with_ends(result, stream_key, least, largest):
    longest = result.shape.index(max(result.shape))
    spots = []
    for shift in (0, 1):
        where = [jax.random.randint(jax.random.fold_in(stream_key, axis), (), 0, length) for axis, length in enumerate(result.shape)]
        where[longest] = (where[longest] + shift) % result.shape[longest]
        spots.append(tuple(where))
    return result.at[spots[0]].set(least).at[spots[1]].set(largest)


def levels(stream_key, shape, split, smallest, high):
    factor_of = 1.0
    for position, parts in split:
        draws = jax.random.uniform(jax.random.fold_in(jax.random.fold_in(stream_key, 6), position), (parts,), jnp.float32, smallest / len(split), high / len(split))
        factor_of = factor_of * jnp.repeat(jnp.exp(draws), shape[position] // parts).reshape((-1,) + (1,) * (len(shape) - 1 - position))
    return factor_of


def scatter_about(rng, shape, deviation, reach, cuts=(), kind=jnp.bfloat16):
    array = jax.random.normal(rng, shape, jnp.float32) * deviation
    if len(cuts) > 0:
        array = levels(rng, shape, cuts, -0.22, 0.18) * array
    return jnp.clip(array, min=-reach, max=reach).astype(kind)


def setup_inputs(seed: int = 0, part: int = 0) -> dict:
    streams_of = jax.random.split(jax.random.key(seed), 7)
    part_splits = jax.random.split(jax.random.fold_in(streams_of[6], part), 7)
    return {
        "queries": draw_queries(jax.random.fold_in(jax.random.fold_in(streams_of[6], part), 71), part),
        "keys": draw_keys(jax.random.fold_in(jax.random.fold_in(streams_of[6], part), 71), part),
        "values": scatter_about(part_splits[2], (SEQ, D), 1.0, 6.0, ((0, 32),)),
        "grad_out": scatter_about(part_splits[3], (SEQ, D), 1.0, 6.0, ((0, 32),)),
        "rand_blocks": with_ends(jax.random.randint(part_splits[4], (SEQ_BLOCKS, RAND), 0, BLOCKS_DEV), jax.random.fold_in(part_splits[4], 1), 0, BLOCKS_DEV - 1).astype(jnp.int32),
        "global_ids": jax.random.randint(part_splits[5], (GLOBALS,), 0, SEQ_BLOCKS).astype(jnp.int32),
    }


SCORE_FLOOR = -1.0e30


def attend_blocks(query_blocks, key_blocks, value_blocks, grad_blocks, key_valid):
    scale_factor = HEAD_DIM ** -0.5
    query_wide = query_blocks.astype(jnp.float32)
    key_wide = key_blocks.astype(jnp.float32)
    value_wide = value_blocks.astype(jnp.float32)
    grad_wide = grad_blocks.astype(jnp.float32)
    scores = jnp.einsum("jqhd,jkhd->jhqk", query_wide, key_wide) * scale_factor
    scores = jnp.where(key_valid[:, None, None, :], scores, SCORE_FLOOR)
    highest = jnp.max(scores, axis=-1, keepdims=True)
    raw_weights = jnp.exp(scores - highest)
    probs = raw_weights / jnp.sum(raw_weights, axis=-1, keepdims=True)
    probs_low = probs.astype(jnp.bfloat16).astype(jnp.float32)
    attended = jnp.einsum("jhqk,jkhd->jqhd", probs_low, value_wide)
    grad_probs = jnp.einsum("jqhd,jkhd->jhqk", grad_wide, value_wide)
    inner = jnp.sum(probs * grad_probs, axis=-1, keepdims=True)
    grad_scores = (scale_factor * probs * (grad_probs - inner)).astype(jnp.bfloat16).astype(jnp.float32)
    grad_query = jnp.einsum("jhqk,jkhd->jqhd", grad_scores, key_wide)
    grad_key = jnp.einsum("jhqk,jqhd->jkhd", grad_scores, query_wide)
    grad_value = jnp.einsum("jhqk,jqhd->jkhd", probs_low, grad_wide)
    return attended, grad_query, grad_key, grad_value


def reference(queries, keys, values, grad_out, rand_blocks, global_ids):
    seq_rows, width = queries.shape
    seq_blocks = seq_rows // BLOCK
    dev_blocks = TOK_DEV // BLOCK
    listed = 3 + GLOBALS + RAND
    block_iota = jnp.arange(seq_blocks, dtype=jnp.int32)
    device_of = block_iota // dev_blocks
    columns = [jnp.clip(block_iota - 1, 0, seq_blocks - 1), block_iota, jnp.clip(block_iota + 1, 0, seq_blocks - 1)]
    for global_slot in range(GLOBALS):
        columns.append(jnp.broadcast_to(global_ids[global_slot], (seq_blocks,)).astype(jnp.int32))
    for matching in range(RAND):
        partner = jnp.bitwise_xor(device_of, jnp.int32(N_CTX // 2 ** (matching + 1)))
        columns.append((partner * dev_blocks + rand_blocks[:, matching]).astype(jnp.int32))
    table = jnp.stack(columns, axis=1).astype(jnp.int32)
    left_ok = block_iota > 0
    right_ok = block_iota < seq_blocks - 1
    stacked = jnp.stack([keys, values]).reshape(2, seq_blocks, BLOCK, width)
    listing_keep = jnp.concatenate([jnp.ones((3,), jnp.float32), jnp.zeros((GLOBALS,), jnp.float32), jnp.ones((RAND,), jnp.float32)])

    def one_slab(carry, slab):
        first = (slab * dev_blocks).astype(jnp.int32)
        rows = lax.dynamic_slice_in_dim(table, first, dev_blocks, 0)
        left_here = lax.dynamic_slice_in_dim(left_ok, first, dev_blocks, 0)
        right_here = lax.dynamic_slice_in_dim(right_ok, first, dev_blocks, 0)
        fill_true = jnp.ones((dev_blocks, BLOCK), dtype=bool)
        key_valid = jnp.concatenate(
            [jnp.broadcast_to(left_here[:, None], (dev_blocks, BLOCK)), fill_true,
             jnp.broadcast_to(right_here[:, None], (dev_blocks, BLOCK)),
             jnp.ones((dev_blocks, (GLOBALS + RAND) * BLOCK), dtype=bool)], axis=1)
        gathered = stacked[:, rows].reshape(2, dev_blocks, listed * BLOCK, HEADS, HEAD_DIM)
        start_row = (slab * TOK_DEV).astype(jnp.int32)
        query_blocks = lax.dynamic_slice_in_dim(queries, start_row, TOK_DEV, 0).reshape(dev_blocks, BLOCK, HEADS, HEAD_DIM)
        grad_blocks = lax.dynamic_slice_in_dim(grad_out, start_row, TOK_DEV, 0).reshape(dev_blocks, BLOCK, HEADS, HEAD_DIM)
        attended, grad_query, grad_key, grad_value = attend_blocks(query_blocks, gathered[0], gathered[1], grad_blocks, key_valid)
        terms = jnp.stack([grad_key, grad_value]).reshape(2, dev_blocks, listed, BLOCK, width)
        terms = terms * listing_keep[None, None, :, None, None]
        carry = carry.at[:, rows].add(terms)
        return carry, (attended.reshape(TOK_DEV, width).astype(jnp.bfloat16), grad_query.reshape(TOK_DEV, width).astype(jnp.bfloat16))

    start = jnp.zeros((2, seq_blocks, BLOCK, width), jnp.float32)
    totals, (attended, grad_query) = lax.scan(one_slab, start, jnp.arange(N_CTX, dtype=jnp.int32))
    grad_keys = totals[0].reshape(seq_rows, width).astype(jnp.bfloat16)
    grad_values = totals[1].reshape(seq_rows, width).astype(jnp.bfloat16)
    return attended.reshape(seq_rows, width), grad_query.reshape(seq_rows, width), grad_keys, grad_values
```

```python
import jax
import jax.numpy as jnp
from jax import lax
from jax.sharding import PartitionSpec as P

HEADS = 16
HEAD_DIM = 64
BLOCK = 64
RAND = 3
GLOBALS = 2


SCORE_FLOOR = -1e30


def padded_2(array, sides, width):
    for axis, dim in sides:
        size, length = (lax.axis_size(axis), array.shape[dim])
        up = [(i, (i + 1) % size) for i in range(size - 1)]
        down = [(j, i) for i, j in up]
        last = lax.slice_in_dim(array, length - width, length, axis=dim)
        first = lax.slice_in_dim(array, 0, width, axis=dim)
        before = lax.ppermute(last, axis, up)
        after = lax.ppermute(first, axis, down)
        array = jnp.concatenate([before, array, after], axis=dim)
    return array


def from_root(blocks, axis, sources):
    size = lax.axis_size(axis)
    position = lax.axis_index(axis)
    shape = (-1,) + (1,) * (blocks.ndim - 1)
    for level in range(size.bit_length() - 1):
        step = 1 << level
        received = lax.ppermute(blocks, axis, [(i, i ^ step) for i in range(size)])
        partner_holds = ((position ^ step) >> level) == (sources >> level)
        blocks = jnp.where(partner_holds.reshape(shape), received, blocks)
    return blocks


def partner_2(array, axis, distance):
    return lax.ppermute(array, axis, [(i, i ^ 1 << distance) for i in range(lax.axis_size(axis))])


def passed_along(array, axis, by):
    size = lax.axis_size(axis)
    pairs = [(i, i + by) for i in range(size) if 0 <= i + by < size]
    return lax.ppermute(array, axis, pairs)


def attend_blocks(query_blocks, key_blocks, value_blocks, grad_blocks, key_valid):
    scale_factor = HEAD_DIM ** (-0.5)
    scores = (
        jnp.einsum("jqhd,jkhd->jhqk", query_blocks, key_blocks, preferred_element_type=jnp.float32)
        * scale_factor
    )
    scores = jnp.where(key_valid[:, None, None, :], scores, SCORE_FLOOR)
    highest = jnp.max(scores, axis=-1, keepdims=True)
    raw_weights = jnp.exp(scores - highest)
    weight_total = jnp.sum(raw_weights, axis=-1, keepdims=True)
    probs = raw_weights / weight_total
    probs_low = probs.astype(jnp.bfloat16)
    attended = jnp.einsum(
        "jhqk,jkhd->jqhd", probs_low, value_blocks, preferred_element_type=jnp.float32
    )
    grad_probs = jnp.einsum(
        "jqhd,jkhd->jhqk", grad_blocks, value_blocks, preferred_element_type=jnp.float32
    )
    inner = jnp.sum(probs * grad_probs, axis=-1, keepdims=True)
    grad_scores = (scale_factor * probs * (grad_probs - inner)).astype(jnp.bfloat16)
    grad_query = jnp.einsum(
        "jhqk,jkhd->jqhd", grad_scores, key_blocks, preferred_element_type=jnp.float32
    )
    grad_key = jnp.einsum(
        "jhqk,jqhd->jkhd", grad_scores, query_blocks, preferred_element_type=jnp.float32
    )
    grad_value = jnp.einsum(
        "jhqk,jqhd->jkhd", probs_low, grad_blocks, preferred_element_type=jnp.float32
    )
    return (attended, grad_query, grad_key, grad_value, (highest, weight_total, inner))


def local(queries, keys, values, grad_out, rand_blocks, global_ids):
    tok_rows, width = queries.shape
    block_count = tok_rows // BLOCK
    listed = 3 + GLOBALS + RAND
    ctx_count = lax.axis_size("ctx")
    position = lax.axis_index("ctx")
    top_bit = ctx_count.bit_length() - 1
    block_iota = jnp.arange(block_count, dtype=jnp.int32)
    stacked = jnp.stack([keys, values])
    padded = padded_2(stacked, (("ctx", 1),), BLOCK)
    framed = padded.reshape(2, block_count + 2, BLOCK, width)
    window = jnp.concatenate([framed[:, :-2], framed[:, 1:-1], framed[:, 2:]], axis=2)
    owners = global_ids // block_count
    local_ids = global_ids % block_count
    own_pieces = jnp.stack(
        [
            lax.dynamic_slice_in_dim(stacked, local_ids[global_slot] * BLOCK, BLOCK, 1)
            for global_slot in range(GLOBALS)
        ],
        axis=1,
    )
    fetched = jnp.swapaxes(from_root(jnp.swapaxes(own_pieces, 0, 1), "ctx", owners), 0, 1)
    global_part = jnp.broadcast_to(
        fetched.reshape(2, 1, GLOBALS * BLOCK, width), (2, block_count, GLOBALS * BLOCK, width)
    )
    pickers = []
    random_parts = []
    for matching in range(RAND):
        spread_bit = top_bit - 1 - matching
        picker = rand_blocks[:, matching][:, None] == block_iota[None, :]
        partner = partner_2(stacked, "ctx", spread_bit).reshape(2, block_count, BLOCK, width)
        chosen = jnp.broadcast_to(partner[:, :1], (2, block_count, BLOCK, width))
        for b in range(1, block_count):
            chosen = jnp.where(picker[None, :, b, None, None], partner[:, b : b + 1], chosen)
        pickers.append(picker)
        random_parts.append(chosen)
    every_key = jnp.concatenate([window, global_part] + random_parts, axis=2)
    key_blocks = every_key[0].reshape(block_count, listed * BLOCK, HEADS, HEAD_DIM)
    value_blocks = every_key[1].reshape(block_count, listed * BLOCK, HEADS, HEAD_DIM)
    global_block = position * block_count + block_iota
    seq_blocks = block_count * ctx_count
    left_ok = global_block > 0
    right_ok = global_block < seq_blocks - 1
    key_valid = jnp.concatenate(
        [
            jnp.broadcast_to(left_ok[:, None], (block_count, BLOCK)),
            jnp.ones((block_count, BLOCK), dtype=bool),
            jnp.broadcast_to(right_ok[:, None], (block_count, BLOCK)),
            jnp.ones((block_count, (GLOBALS + RAND) * BLOCK), dtype=bool),
        ],
        axis=1,
    )
    query_blocks = queries.reshape(block_count, BLOCK, HEADS, HEAD_DIM)
    grad_blocks = grad_out.reshape(block_count, BLOCK, HEADS, HEAD_DIM)
    attended, grad_query, grad_key, grad_value, softmax_stats = attend_blocks(
        query_blocks, key_blocks, value_blocks, grad_blocks, key_valid
    )
    split = jnp.stack([grad_key, grad_value]).reshape(2, block_count, listed, BLOCK, width)
    own_window = (
        jnp.pad(split[:, :, 0], ((0, 0), (0, 2), (0, 0), (0, 0)))
        + jnp.pad(split[:, :, 1], ((0, 0), (1, 1), (0, 0), (0, 0)))
        + jnp.pad(split[:, :, 2], ((0, 0), (2, 0), (0, 0), (0, 0)))
    )
    from_right = passed_along(own_window[:, 0], "ctx", -1)
    from_left = passed_along(own_window[:, -1], "ctx", 1)
    own_total = own_window[:, 1:-1]
    own_total = own_total.at[:, -1].add(from_right)
    own_total = own_total.at[:, 0].add(from_left)
    for matching in range(RAND):
        spread_bit = top_bit - 1 - matching
        terms = split[:, :, 3 + GLOBALS + matching]
        routed = sum(
            jnp.where(pickers[matching][None, j, :, None, None], terms[:, j : j + 1], 0.0)
            for j in range(block_count)
        )
        own_total = own_total + partner_2(routed, "ctx", spread_bit)
    attended_out = attended.reshape(tok_rows, width).astype(jnp.bfloat16)
    grad_queries = grad_query.reshape(tok_rows, width).astype(jnp.bfloat16)
    grad_keys = own_total[0].reshape(tok_rows, width).astype(jnp.bfloat16)
    grad_values = own_total[1].reshape(tok_rows, width).astype(jnp.bfloat16)
    return (attended_out, grad_queries, grad_keys, grad_values)


def solution(mesh):
    placed = (
        P(("dp", "ctx"), None),
        P(("dp", "ctx"), None),
        P(("dp", "ctx"), None),
        P(("dp", "ctx"), None),
        P(("dp", "ctx"), None),
        P("dp"),
    )
    return jax.shard_map(
        local,
        mesh=mesh,
        in_specs=placed,
        out_specs=(
            P(("dp", "ctx"), None),
            P(("dp", "ctx"), None),
            P(("dp", "ctx"), None),
            P(("dp", "ctx"), None),
        ),
        check_vma=False,
    )
```

```python
import jax
import jax.numpy as jnp
from jax import lax
from jax.sharding import PartitionSpec as P

HEADS = 16
HEAD_DIM = 64
BLOCK = 64
RAND = 3
GLOBALS = 2


SCORE_FLOOR = -1e30


def padded_2(array, sides, width):
    for axis, dim in sides:
        size, length = (lax.axis_size(axis), array.shape[dim])
        up = [(i, (i + 1) % size) for i in range(size - 1)]
        down = [(j, i) for i, j in up]
        last = lax.slice_in_dim(array, length - width, length, axis=dim)
        first = lax.slice_in_dim(array, 0, width, axis=dim)
        before = lax.ppermute(last, axis, up)
        after = lax.ppermute(first, axis, down)
        array = jnp.concatenate([before, array, after], axis=dim)
    return array


def from_root(blocks, axis, sources):
    size = lax.axis_size(axis)
    position = lax.axis_index(axis)
    shape = (-1,) + (1,) * (blocks.ndim - 2)
    core = position % 2
    sibling = [(i, i ^ 1) for i in range(size)]
    mine = jnp.where(core == 0, blocks[:, 0], blocks[:, 1])
    theirs = jnp.where(core == 0, blocks[:, 1], blocks[:, 0])
    received = lax.ppermute(theirs, axis, sibling)
    carried = jnp.where((sources == (position ^ 1)).reshape(shape), received, mine)
    for level in range(1, size.bit_length() - 1):
        step = 1 << level
        received = lax.ppermute(carried, axis, [(i, i ^ step) for i in range(size)])
        partner_holds = ((position ^ step) >> level) == (sources >> level)
        carried = jnp.where(partner_holds.reshape(shape), received, carried)
    other = lax.ppermute(carried, axis, sibling)
    first = jnp.where(core == 0, carried, other)
    second = jnp.where(core == 0, other, carried)
    return jnp.stack([first, second], axis=1)


def partner_2(array, axis, distance):
    return lax.ppermute(array, axis, [(i, i ^ 1 << distance) for i in range(lax.axis_size(axis))])


def passed_along(array, axis, by):
    size = lax.axis_size(axis)
    pairs = [(i, i + by) for i in range(size) if 0 <= i + by < size]
    return lax.ppermute(array, axis, pairs)


def attend_blocks(query_blocks, key_blocks, value_blocks, grad_blocks, key_valid):
    scale_factor = HEAD_DIM ** (-0.5)
    scores = (
        jnp.einsum("jqhd,jkhd->jhqk", query_blocks, key_blocks, preferred_element_type=jnp.float32)
        * scale_factor
    )
    scores = jnp.where(key_valid[:, None, None, :], scores, SCORE_FLOOR)
    highest = jnp.max(scores, axis=-1, keepdims=True)
    raw_weights = jnp.exp(scores - highest)
    weight_total = jnp.sum(raw_weights, axis=-1, keepdims=True)
    probs = raw_weights / weight_total
    probs_low = probs.astype(jnp.bfloat16)
    attended = jnp.einsum(
        "jhqk,jkhd->jqhd", probs_low, value_blocks, preferred_element_type=jnp.float32
    )
    grad_probs = jnp.einsum(
        "jqhd,jkhd->jhqk", grad_blocks, value_blocks, preferred_element_type=jnp.float32
    )
    inner = jnp.sum(probs * grad_probs, axis=-1, keepdims=True)
    grad_scores = (scale_factor * probs * (grad_probs - inner)).astype(jnp.bfloat16)
    grad_query = jnp.einsum(
        "jhqk,jkhd->jqhd", grad_scores, key_blocks, preferred_element_type=jnp.float32
    )
    grad_key = jnp.einsum(
        "jhqk,jqhd->jkhd", grad_scores, query_blocks, preferred_element_type=jnp.float32
    )
    grad_value = jnp.einsum(
        "jhqk,jqhd->jkhd", probs_low, grad_blocks, preferred_element_type=jnp.float32
    )
    return (attended, grad_query, grad_key, grad_value, (highest, weight_total, inner))


def local(queries, keys, values, grad_out, rand_blocks, global_ids):
    tok_rows, width = queries.shape
    block_count = tok_rows // BLOCK
    listed = 3 + GLOBALS + RAND
    ctx_count = lax.axis_size("ctx")
    position = lax.axis_index("ctx")
    top_bit = ctx_count.bit_length() - 1
    block_iota = jnp.arange(block_count, dtype=jnp.int32)
    stacked = jnp.stack([keys, values])
    padded = padded_2(stacked, (("ctx", 1),), BLOCK)
    framed = padded.reshape(2, block_count + 2, BLOCK, width)
    window = jnp.concatenate([framed[:, :-2], framed[:, 1:-1], framed[:, 2:]], axis=2)
    owners = global_ids // block_count
    local_ids = global_ids % block_count
    own_pieces = jnp.stack(
        [
            lax.dynamic_slice_in_dim(stacked, local_ids[global_slot] * BLOCK, BLOCK, 1)
            for global_slot in range(GLOBALS)
        ],
        axis=1,
    )
    fetched = jnp.swapaxes(from_root(jnp.swapaxes(own_pieces, 0, 1), "ctx", owners), 0, 1)
    global_part = jnp.broadcast_to(
        fetched.reshape(2, 1, GLOBALS * BLOCK, width), (2, block_count, GLOBALS * BLOCK, width)
    )
    pickers = []
    random_parts = []
    for matching in range(RAND):
        spread_bit = top_bit - 1 - matching
        picker = rand_blocks[:, matching][:, None] == block_iota[None, :]
        partner = partner_2(stacked, "ctx", spread_bit).reshape(2, block_count, BLOCK, width)
        chosen = jnp.broadcast_to(partner[:, :1], (2, block_count, BLOCK, width))
        for b in range(1, block_count):
            chosen = jnp.where(picker[None, :, b, None, None], partner[:, b : b + 1], chosen)
        pickers.append(picker)
        random_parts.append(chosen)
    every_key = jnp.concatenate([window, global_part] + random_parts, axis=2)
    key_blocks = every_key[0].reshape(block_count, listed * BLOCK, HEADS, HEAD_DIM)
    value_blocks = every_key[1].reshape(block_count, listed * BLOCK, HEADS, HEAD_DIM)
    global_block = position * block_count + block_iota
    seq_blocks = block_count * ctx_count
    left_ok = global_block > 0
    right_ok = global_block < seq_blocks - 1
    key_valid = jnp.concatenate(
        [
            jnp.broadcast_to(left_ok[:, None], (block_count, BLOCK)),
            jnp.ones((block_count, BLOCK), dtype=bool),
            jnp.broadcast_to(right_ok[:, None], (block_count, BLOCK)),
            jnp.ones((block_count, (GLOBALS + RAND) * BLOCK), dtype=bool),
        ],
        axis=1,
    )
    query_blocks = queries.reshape(block_count, BLOCK, HEADS, HEAD_DIM)
    grad_blocks = grad_out.reshape(block_count, BLOCK, HEADS, HEAD_DIM)
    attended, grad_query, grad_key, grad_value, softmax_stats = attend_blocks(
        query_blocks, key_blocks, value_blocks, grad_blocks, key_valid
    )
    split = jnp.stack([grad_key, grad_value]).reshape(2, block_count, listed, BLOCK, width)
    own_window = (
        jnp.pad(split[:, :, 0], ((0, 0), (0, 2), (0, 0), (0, 0)))
        + jnp.pad(split[:, :, 1], ((0, 0), (1, 1), (0, 0), (0, 0)))
        + jnp.pad(split[:, :, 2], ((0, 0), (2, 0), (0, 0), (0, 0)))
    )
    from_right = passed_along(own_window[:, 0], "ctx", -1)
    from_left = passed_along(own_window[:, -1], "ctx", 1)
    own_total = own_window[:, 1:-1]
    own_total = own_total.at[:, -1].add(from_right)
    own_total = own_total.at[:, 0].add(from_left)
    for matching in range(RAND):
        spread_bit = top_bit - 1 - matching
        terms = split[:, :, 3 + GLOBALS + matching]
        routed = sum(
            jnp.where(pickers[matching][None, j, :, None, None], terms[:, j : j + 1], 0.0)
            for j in range(block_count)
        )
        own_total = own_total + partner_2(routed, "ctx", spread_bit)
    attended_out = attended.reshape(tok_rows, width).astype(jnp.bfloat16)
    grad_queries = grad_query.reshape(tok_rows, width).astype(jnp.bfloat16)
    grad_keys = own_total[0].reshape(tok_rows, width).astype(jnp.bfloat16)
    grad_values = own_total[1].reshape(tok_rows, width).astype(jnp.bfloat16)
    return (attended_out, grad_queries, grad_keys, grad_values)


def solution(mesh):
    placed = (
        P(("dp", "ctx"), None),
        P(("dp", "ctx"), None),
        P(("dp", "ctx"), None),
        P(("dp", "ctx"), None),
        P(("dp", "ctx"), None),
        P("dp"),
    )
    return jax.shard_map(
        local,
        mesh=mesh,
        in_specs=placed,
        out_specs=(
            P(("dp", "ctx"), None),
            P(("dp", "ctx"), None),
            P(("dp", "ctx"), None),
            P(("dp", "ctx"), None),
        ),
        check_vma=False,
    )
```

```python
import jax
import jax.numpy as jnp
from jax import lax
from jax.sharding import PartitionSpec as P

HEADS = 16
HEAD_DIM = 64
BLOCK = 64
RAND = 3
GLOBALS = 2


SCORE_FLOOR = -1e30


def padded_2(array, sides, width):
    for axis, dim in sides:
        size, length = (lax.axis_size(axis), array.shape[dim])
        up = [(i, (i + 1) % size) for i in range(size - 1)]
        down = [(j, i) for i, j in up]
        last = lax.slice_in_dim(array, length - width, length, axis=dim)
        first = lax.slice_in_dim(array, 0, width, axis=dim)
        before = lax.ppermute(last, axis, up)
        after = lax.ppermute(first, axis, down)
        array = jnp.concatenate([before, array, after], axis=dim)
    return array


def from_root(blocks, axis, sources):
    size = lax.axis_size(axis)
    position = lax.axis_index(axis)
    shape = (-1,) + (1,) * (blocks.ndim - 2)
    core = position % 2
    sibling = [(i, i ^ 1) for i in range(size)]
    mine = jnp.where(core == 0, blocks[:, 0], blocks[:, 1])
    theirs = jnp.where(core == 0, blocks[:, 1], blocks[:, 0])
    received = lax.ppermute(theirs, axis, sibling)
    carried = jnp.where((sources == (position ^ 1)).reshape(shape), received, mine)
    for level in range(1, size.bit_length() - 1):
        step = 1 << level
        received = lax.ppermute(carried, axis, [(i, i ^ step) for i in range(size)])
        partner_holds = ((position ^ step) >> level) == (sources >> level)
        carried = jnp.where(partner_holds.reshape(shape), received, carried)
    other = lax.ppermute(carried, axis, sibling)
    first = jnp.where(core == 0, carried, other)
    second = jnp.where(core == 0, other, carried)
    return jnp.stack([first, second], axis=1)


def partner_2(array, axis, distance):
    return lax.ppermute(array, axis, [(i, i ^ 1 << distance) for i in range(lax.axis_size(axis))])


def passed_along(array, axis, by):
    size = lax.axis_size(axis)
    pairs = [(i, i + by) for i in range(size) if 0 <= i + by < size]
    return lax.ppermute(array, axis, pairs)


def attend_blocks(query_blocks, key_blocks, value_blocks, grad_blocks, key_valid):
    scale_factor = HEAD_DIM ** (-0.5)
    scores = (
        jnp.einsum("jqhd,jkhd->jhqk", query_blocks, key_blocks, preferred_element_type=jnp.float32)
        * scale_factor
    )
    scores = jnp.where(key_valid[:, None, None, :], scores, SCORE_FLOOR)
    highest = jnp.max(scores, axis=-1, keepdims=True)
    raw_weights = jnp.exp(scores - highest)
    weight_total = jnp.sum(raw_weights, axis=-1, keepdims=True)
    probs = raw_weights / weight_total
    probs_low = probs.astype(jnp.bfloat16)
    attended = jnp.einsum(
        "jhqk,jkhd->jqhd", probs_low, value_blocks, preferred_element_type=jnp.float32
    )
    grad_probs = jnp.einsum(
        "jqhd,jkhd->jhqk", grad_blocks, value_blocks, preferred_element_type=jnp.float32
    )
    inner = jnp.sum(probs * grad_probs, axis=-1, keepdims=True)
    grad_scores = (scale_factor * probs * (grad_probs - inner)).astype(jnp.bfloat16)
    grad_query = jnp.einsum(
        "jhqk,jkhd->jqhd", grad_scores, key_blocks, preferred_element_type=jnp.float32
    )
    grad_key = jnp.einsum(
        "jhqk,jqhd->jkhd", grad_scores, query_blocks, preferred_element_type=jnp.float32
    )
    grad_value = jnp.einsum(
        "jhqk,jqhd->jkhd", probs_low, grad_blocks, preferred_element_type=jnp.float32
    )
    return (attended, grad_query, grad_key, grad_value, (highest, weight_total, inner))


def local(queries, keys, values, grad_out, rand_blocks, global_ids):
    tok_rows, width = queries.shape
    block_count = tok_rows // BLOCK
    listed = 3 + GLOBALS + RAND
    ctx_count = lax.axis_size("ctx")
    position = lax.axis_index("ctx")
    top_bit = ctx_count.bit_length() - 1
    block_iota = jnp.arange(block_count, dtype=jnp.int32)
    stacked = jnp.stack([keys, values])
    padded = padded_2(stacked, (("ctx", 1),), BLOCK)
    framed = padded.reshape(2, block_count + 2, BLOCK, width)
    window = jnp.concatenate([framed[:, :-2], framed[:, 1:-1], framed[:, 2:]], axis=2)
    owners = global_ids // block_count
    local_ids = global_ids % block_count
    own_pieces = jnp.stack(
        [
            lax.dynamic_slice_in_dim(stacked, local_ids[global_slot] * BLOCK, BLOCK, 1)
            for global_slot in range(GLOBALS)
        ],
        axis=1,
    )
    fetched = jnp.swapaxes(from_root(jnp.swapaxes(own_pieces, 0, 1), "ctx", owners), 0, 1)
    global_part = jnp.broadcast_to(
        fetched.reshape(2, 1, GLOBALS * BLOCK, width), (2, block_count, GLOBALS * BLOCK, width)
    )
    pickers = []
    random_parts = []
    for matching in range(RAND):
        spread_bit = top_bit - 1 - matching
        picker = rand_blocks[:, matching][:, None] == block_iota[None, :]
        partner = partner_2(stacked, "ctx", spread_bit).reshape(2, block_count, BLOCK, width)
        chosen = jnp.broadcast_to(partner[:, :1], (2, block_count, BLOCK, width))
        for b in range(1, block_count):
            chosen = jnp.where(picker[None, :, b, None, None], partner[:, b : b + 1], chosen)
        pickers.append(picker)
        random_parts.append(chosen)
    every_key = jnp.concatenate([window, global_part] + random_parts, axis=2)
    key_blocks = every_key[0].reshape(block_count, listed * BLOCK, HEADS, HEAD_DIM)
    value_blocks = every_key[1].reshape(block_count, listed * BLOCK, HEADS, HEAD_DIM)
    global_block = position * block_count + block_iota
    seq_blocks = block_count * ctx_count
    left_ok = global_block > 0
    right_ok = global_block < seq_blocks - 1
    key_valid = jnp.concatenate(
        [
            jnp.broadcast_to(left_ok[:, None], (block_count, BLOCK)),
            jnp.ones((block_count, BLOCK), dtype=bool),
            jnp.broadcast_to(right_ok[:, None], (block_count, BLOCK)),
            jnp.ones((block_count, (GLOBALS + RAND) * BLOCK), dtype=bool),
        ],
        axis=1,
    )
    query_blocks = queries.reshape(block_count, BLOCK, HEADS, HEAD_DIM)
    grad_blocks = grad_out.reshape(block_count, BLOCK, HEADS, HEAD_DIM)
    attended, grad_query, grad_key, grad_value, softmax_stats = attend_blocks(
        query_blocks, key_blocks, value_blocks, grad_blocks, key_valid
    )
    split = jnp.stack([grad_key, grad_value]).reshape(2, block_count, listed, BLOCK, width)
    own_window = (
        jnp.pad(split[:, :, 0], ((0, 0), (0, 2), (0, 0), (0, 0)))
        + jnp.pad(split[:, :, 1], ((0, 0), (1, 1), (0, 0), (0, 0)))
        + jnp.pad(split[:, :, 2], ((0, 0), (2, 0), (0, 0), (0, 0)))
    )
    low = jnp.bfloat16
    from_right = passed_along(own_window[:, 0].astype(low), "ctx", -1).astype(jnp.float32)
    from_left = passed_along(own_window[:, -1].astype(low), "ctx", 1).astype(jnp.float32)
    own_total = own_window[:, 1:-1]
    own_total = own_total.at[:, -1].add(from_right)
    own_total = own_total.at[:, 0].add(from_left)
    for matching in range(RAND):
        spread_bit = top_bit - 1 - matching
        terms = split[:, :, 3 + GLOBALS + matching]
        routed = sum(
            jnp.where(pickers[matching][None, j, :, None, None], terms[:, j : j + 1], 0.0)
            for j in range(block_count)
        )
        own_total = own_total + partner_2(routed.astype(low), "ctx", spread_bit).astype(jnp.float32)
    attended_out = attended.reshape(tok_rows, width).astype(jnp.bfloat16)
    grad_queries = grad_query.reshape(tok_rows, width).astype(jnp.bfloat16)
    grad_keys = own_total[0].reshape(tok_rows, width).astype(jnp.bfloat16)
    grad_values = own_total[1].reshape(tok_rows, width).astype(jnp.bfloat16)
    return (attended_out, grad_queries, grad_keys, grad_values)


def solution(mesh):
    placed = (
        P(("dp", "ctx"), None),
        P(("dp", "ctx"), None),
        P(("dp", "ctx"), None),
        P(("dp", "ctx"), None),
        P(("dp", "ctx"), None),
        P("dp"),
    )
    return jax.shard_map(
        local,
        mesh=mesh,
        in_specs=placed,
        out_specs=(
            P(("dp", "ctx"), None),
            P(("dp", "ctx"), None),
            P(("dp", "ctx"), None),
            P(("dp", "ctx"), None),
        ),
        check_vma=False,
    )
```

```python
import jax
import jax.numpy as jnp
from jax import lax
from jax.sharding import PartitionSpec as P
from jax.experimental import pallas as pl
from jax.experimental.pallas import tpu as pltpu

HEADS = 16
HEAD_DIM = 64
BLOCK = 64
RAND = 3
GLOBALS = 2


SCORE_FLOOR = -1e30


def padded_2(array, sides, width):
    for axis, dim in sides:
        size, length = (lax.axis_size(axis), array.shape[dim])
        up = [(i, (i + 1) % size) for i in range(size - 1)]
        down = [(j, i) for i, j in up]
        last = lax.slice_in_dim(array, length - width, length, axis=dim)
        first = lax.slice_in_dim(array, 0, width, axis=dim)
        before = lax.ppermute(last, axis, up)
        after = lax.ppermute(first, axis, down)
        array = jnp.concatenate([before, array, after], axis=dim)
    return array


def from_root(blocks, axis, sources):
    size = lax.axis_size(axis)
    position = lax.axis_index(axis)
    shape = (-1,) + (1,) * (blocks.ndim - 2)
    core = position % 2
    sibling = [(i, i ^ 1) for i in range(size)]
    mine = jnp.where(core == 0, blocks[:, 0], blocks[:, 1])
    theirs = jnp.where(core == 0, blocks[:, 1], blocks[:, 0])
    received = lax.ppermute(theirs, axis, sibling)
    carried = jnp.where((sources == (position ^ 1)).reshape(shape), received, mine)
    for level in range(1, size.bit_length() - 1):
        step = 1 << level
        received = lax.ppermute(carried, axis, [(i, i ^ step) for i in range(size)])
        partner_holds = ((position ^ step) >> level) == (sources >> level)
        carried = jnp.where(partner_holds.reshape(shape), received, carried)
    other = lax.ppermute(carried, axis, sibling)
    first = jnp.where(core == 0, carried, other)
    second = jnp.where(core == 0, other, carried)
    return jnp.stack([first, second], axis=1)


def partner_2(array, axis, distance):
    return lax.ppermute(array, axis, [(i, i ^ 1 << distance) for i in range(lax.axis_size(axis))])


def passed_along(array, axis, by):
    size = lax.axis_size(axis)
    pairs = [(i, i + by) for i in range(size) if 0 <= i + by < size]
    return lax.ppermute(array, axis, pairs)


LANES = 128


def attend_kernel(meta_ref, q_ref, g_ref, win_ref, glob_ref, *rest):
    partner_refs = rest[:RAND]
    att_ref, gq_ref, gwin_ref, gpart_ref = rest[RAND:]
    block_count = q_ref.shape[0] // BLOCK
    listed = 3 + GLOBALS + RAND
    scale_factor = HEAD_DIM ** (-0.5)
    gwin_ref[...] = jnp.zeros_like(gwin_ref)
    gpart_ref[...] = jnp.zeros_like(gpart_ref)
    lane = lax.broadcasted_iota(jnp.int32, (BLOCK, LANES), 1)
    col = lax.broadcasted_iota(jnp.int32, (BLOCK, listed * BLOCK), 1)
    nt = (((1,), (1,)), ((), ()))
    tn = (((0,), (0,)), ((), ()))
    base = (3 + GLOBALS) * BLOCK
    for j in range(block_count):
        rows = pl.ds(j * BLOCK, BLOCK)
        q = q_ref[rows, :]
        g = g_ref[rows, :]
        picks = [pl.multiple_of(meta_ref[j * RAND + r] * BLOCK, BLOCK) for r in range(RAND)]
        left_ok = meta_ref[block_count * RAND + j]
        right_ok = meta_ref[block_count * RAND + block_count + j]

        def gather(kv):
            parts = [win_ref[kv, pl.ds(j * BLOCK, 3 * BLOCK), :], glob_ref[kv]]
            for r in range(RAND):
                parts.append(partner_refs[r][kv, pl.ds(picks[r], BLOCK), :])
            return jnp.concatenate(parts, axis=0)

        k = gather(0)
        v = gather(1)
        invalid = ((col < BLOCK) & (left_ok == 0)) | (
            (col >= 2 * BLOCK) & (col < 3 * BLOCK) & (right_ok == 0)
        )
        att = jnp.zeros((BLOCK, LANES), jnp.float32)
        gq = jnp.zeros((BLOCK, LANES), jnp.float32)
        gk = jnp.zeros((listed * BLOCK, LANES), jnp.float32)
        gv = jnp.zeros((listed * BLOCK, LANES), jnp.float32)
        for h in range(LANES // HEAD_DIM):
            in_head = (lane >= h * HEAD_DIM) & (lane < (h + 1) * HEAD_DIM)
            qh = jnp.where(in_head, q, jnp.zeros_like(q))
            gh = jnp.where(in_head, g, jnp.zeros_like(g))
            scores = lax.dot_general(qh, k, nt, preferred_element_type=jnp.float32) * scale_factor
            scores = jnp.where(invalid, SCORE_FLOOR, scores)
            highest = jnp.max(scores, axis=-1, keepdims=True)
            raw_weights = jnp.exp(scores - highest)
            weight_total = jnp.sum(raw_weights, axis=-1, keepdims=True)
            probs = raw_weights / weight_total
            probs_low = probs.astype(jnp.bfloat16)
            att = jnp.where(
                in_head, jnp.dot(probs_low, v, preferred_element_type=jnp.float32), att
            )
            grad_probs = lax.dot_general(gh, v, nt, preferred_element_type=jnp.float32)
            inner = jnp.sum(probs * grad_probs, axis=-1, keepdims=True)
            grad_scores = (scale_factor * probs * (grad_probs - inner)).astype(jnp.bfloat16)
            gq = jnp.where(
                in_head, jnp.dot(grad_scores, k, preferred_element_type=jnp.float32), gq
            )
            gk = gk + lax.dot_general(grad_scores, qh, tn, preferred_element_type=jnp.float32)
            gv = gv + lax.dot_general(probs_low, gh, tn, preferred_element_type=jnp.float32)
        att_ref[rows, :] = att.astype(att_ref.dtype)
        gq_ref[rows, :] = gq.astype(gq_ref.dtype)
        window = pl.ds(j * BLOCK, 3 * BLOCK)
        gwin_ref[0, window, :] += gk[: 3 * BLOCK]
        gwin_ref[1, window, :] += gv[: 3 * BLOCK]
        for r in range(RAND):
            there = pl.ds(picks[r], BLOCK)
            gpart_ref[r, 0, there, :] += gk[base + r * BLOCK : base + (r + 1) * BLOCK]
            gpart_ref[r, 1, there, :] += gv[base + r * BLOCK : base + (r + 1) * BLOCK]


def attend(meta, queries, grad_out, padded, glob, partners):
    tok_rows, width = queries.shape
    framed = padded.shape[1]
    pairs = width // LANES
    row_spec = pl.BlockSpec((tok_rows, LANES), lambda p, m: (0, p))
    win_spec = pl.BlockSpec((2, framed, LANES), lambda p, m: (0, 0, p))
    glob_spec = pl.BlockSpec((2, glob.shape[1], LANES), lambda p, m: (0, 0, p))
    part_spec = pl.BlockSpec((2, tok_rows, LANES), lambda p, m: (0, 0, p))
    out_specs = [
        row_spec,
        row_spec,
        win_spec,
        pl.BlockSpec((RAND, 2, tok_rows, LANES), lambda p, m: (0, 0, 0, p)),
    ]
    out_shape = [
        jax.ShapeDtypeStruct((tok_rows, width), jnp.bfloat16),
        jax.ShapeDtypeStruct((tok_rows, width), jnp.bfloat16),
        jax.ShapeDtypeStruct((2, framed, width), jnp.float32),
        jax.ShapeDtypeStruct((RAND, 2, tok_rows, width), jnp.float32),
    ]
    return pl.pallas_call(
        attend_kernel,
        grid_spec=pltpu.PrefetchScalarGridSpec(
            num_scalar_prefetch=1,
            grid=(pairs,),
            in_specs=[row_spec, row_spec, win_spec, glob_spec] + [part_spec] * RAND,
            out_specs=out_specs,
        ),
        out_shape=out_shape,
        compiler_params=pltpu.CompilerParams(dimension_semantics=("arbitrary",)),
    )(meta, queries, grad_out, padded, glob, *partners)


def local(queries, keys, values, grad_out, rand_blocks, global_ids):
    tok_rows, width = queries.shape
    block_count = tok_rows // BLOCK
    ctx_count = lax.axis_size("ctx")
    position = lax.axis_index("ctx")
    top_bit = ctx_count.bit_length() - 1
    block_iota = jnp.arange(block_count, dtype=jnp.int32)
    stacked = jnp.stack([keys, values])
    padded = padded_2(stacked, (("ctx", 1),), BLOCK)
    owners = global_ids // block_count
    local_ids = global_ids % block_count
    own_pieces = jnp.stack(
        [
            lax.dynamic_slice_in_dim(stacked, local_ids[global_slot] * BLOCK, BLOCK, 1)
            for global_slot in range(GLOBALS)
        ],
        axis=1,
    )
    fetched = jnp.swapaxes(from_root(jnp.swapaxes(own_pieces, 0, 1), "ctx", owners), 0, 1)
    glob = fetched.reshape(2, GLOBALS * BLOCK, width)
    spread = [top_bit - 1 - matching for matching in range(RAND)]
    partners = [partner_2(stacked, "ctx", bit) for bit in spread]
    global_block = position * block_count + block_iota
    seq_blocks = block_count * ctx_count
    meta = jnp.concatenate(
        [
            rand_blocks.reshape(-1).astype(jnp.int32),
            (global_block > 0).astype(jnp.int32),
            (global_block < seq_blocks - 1).astype(jnp.int32),
        ]
    )
    attended_out, grad_queries, gwin, gpart = attend(
        meta, queries, grad_out, padded, glob, partners
    )
    low = jnp.bfloat16
    from_right = passed_along(gwin[:, :BLOCK].astype(low), "ctx", -1).astype(jnp.float32)
    from_left = passed_along(gwin[:, -BLOCK:].astype(low), "ctx", 1).astype(jnp.float32)
    own_total = gwin[:, BLOCK:-BLOCK]
    own_total = own_total.at[:, tok_rows - BLOCK :].add(from_right)
    own_total = own_total.at[:, :BLOCK].add(from_left)
    for matching in range(RAND):
        own_total = own_total + partner_2(gpart[matching].astype(low), "ctx", spread[matching]).astype(
            jnp.float32
        )
    grad_keys = own_total[0].astype(jnp.bfloat16)
    grad_values = own_total[1].astype(jnp.bfloat16)
    return (attended_out, grad_queries, grad_keys, grad_values)


def solution(mesh):
    placed = (
        P(("dp", "ctx"), None),
        P(("dp", "ctx"), None),
        P(("dp", "ctx"), None),
        P(("dp", "ctx"), None),
        P(("dp", "ctx"), None),
        P("dp"),
    )
    return jax.shard_map(
        local,
        mesh=mesh,
        in_specs=placed,
        out_specs=(
            P(("dp", "ctx"), None),
            P(("dp", "ctx"), None),
            P(("dp", "ctx"), None),
            P(("dp", "ctx"), None),
        ),
        check_vma=False,
    )
```

```python
import jax
import jax.numpy as jnp
from jax import lax
from jax.sharding import PartitionSpec as P
from jax.experimental import pallas as pl
from jax.experimental.pallas import tpu as pltpu

HEADS = 16
HEAD_DIM = 64
BLOCK = 64
RAND = 3
GLOBALS = 2


SCORE_FLOOR = -1e30


def padded_2(array, sides, width):
    for axis, dim in sides:
        size, length = (lax.axis_size(axis), array.shape[dim])
        up = [(i, (i + 1) % size) for i in range(size - 1)]
        down = [(j, i) for i, j in up]
        last = lax.slice_in_dim(array, length - width, length, axis=dim)
        first = lax.slice_in_dim(array, 0, width, axis=dim)
        before = lax.ppermute(last, axis, up)
        after = lax.ppermute(first, axis, down)
        array = jnp.concatenate([before, array, after], axis=dim)
    return array


def from_root(blocks, axis, sources, mask):
    size = lax.axis_size(axis)
    position = lax.axis_index(axis)
    shape = (-1,) + (1,) * (blocks.ndim - 2)
    core = position % 2
    sibling = [(i, i ^ 1) for i in range(size)]

    def holds(partner):
        return (((sources ^ partner) & ~mask) == 0).reshape(shape)

    mine = jnp.where(core == 0, blocks[:, 0], blocks[:, 1])
    theirs = jnp.where(core == 0, blocks[:, 1], blocks[:, 0])
    received = lax.ppermute(theirs, axis, sibling)
    carried = jnp.where(holds(position ^ 1), received, mine)
    mask = mask | 1
    for level in range(1, size.bit_length() - 1):
        step = 1 << level
        if mask & step:
            continue
        received = lax.ppermute(carried, axis, [(i, i ^ step) for i in range(size)])
        carried = jnp.where(holds(position ^ step), received, carried)
        mask = mask | step
    other = lax.ppermute(carried, axis, sibling)
    first = jnp.where(core == 0, carried, other)
    second = jnp.where(core == 0, other, carried)
    return jnp.stack([first, second], axis=1)


def partner_2(array, axis, distance):
    return lax.ppermute(array, axis, [(i, i ^ 1 << distance) for i in range(lax.axis_size(axis))])


def passed_along(array, axis, by):
    size = lax.axis_size(axis)
    pairs = [(i, i + by) for i in range(size) if 0 <= i + by < size]
    return lax.ppermute(array, axis, pairs)


LANES = 128


def attend_kernel(meta_ref, q_ref, g_ref, win_ref, glob_ref, *rest):
    partner_refs = rest[:RAND]
    att_ref, gq_ref, gwin_ref, gpart_ref = rest[RAND:]
    block_count = q_ref.shape[0] // BLOCK
    listed = 3 + GLOBALS + RAND
    scale_factor = HEAD_DIM ** (-0.5)
    gwin_ref[...] = jnp.zeros_like(gwin_ref)
    gpart_ref[...] = jnp.zeros_like(gpart_ref)
    lane = lax.broadcasted_iota(jnp.int32, (BLOCK, LANES), 1)
    per_pair = LANES // HEAD_DIM
    col = lax.broadcasted_iota(jnp.int32, (per_pair * BLOCK, listed * BLOCK), 1)
    nt = (((1,), (1,)), ((), ()))
    tn = (((0,), (0,)), ((), ()))
    base = (3 + GLOBALS) * BLOCK
    for j in range(block_count):
        rows = pl.ds(j * BLOCK, BLOCK)
        q = q_ref[rows, :]
        g = g_ref[rows, :]
        picks = [pl.multiple_of(meta_ref[j * RAND + r] * BLOCK, BLOCK) for r in range(RAND)]
        left_ok = meta_ref[block_count * RAND + j]
        right_ok = meta_ref[block_count * RAND + block_count + j]

        def gather(kv):
            parts = [win_ref[kv, pl.ds(j * BLOCK, 3 * BLOCK), :], glob_ref[kv]]
            for r in range(RAND):
                parts.append(partner_refs[r][kv, pl.ds(picks[r], BLOCK), :])
            return jnp.concatenate(parts, axis=0)

        k = gather(0)
        v = gather(1)
        invalid = ((col < BLOCK) & (left_ok == 0)) | (
            (col >= 2 * BLOCK) & (col < 3 * BLOCK) & (right_ok == 0)
        )
        heads = [(lane >= h * HEAD_DIM) & (lane < (h + 1) * HEAD_DIM) for h in range(per_pair)]
        qm = jnp.concatenate([jnp.where(m, q, jnp.zeros_like(q)) for m in heads], axis=0)
        gm = jnp.concatenate([jnp.where(m, g, jnp.zeros_like(g)) for m in heads], axis=0)
        scores = lax.dot_general(qm, k, nt, preferred_element_type=jnp.float32) * scale_factor
        scores = jnp.where(invalid, SCORE_FLOOR, scores)
        highest = jnp.max(scores, axis=-1, keepdims=True)
        raw_weights = jnp.exp(scores - highest)
        weight_total = jnp.sum(raw_weights, axis=-1, keepdims=True)
        probs = raw_weights / weight_total
        probs_low = probs.astype(jnp.bfloat16)
        grad_probs = lax.dot_general(gm, v, nt, preferred_element_type=jnp.float32)
        inner = jnp.sum(probs * grad_probs, axis=-1, keepdims=True)
        grad_scores = (scale_factor * probs * (grad_probs - inner)).astype(jnp.bfloat16)
        att_all = jnp.dot(probs_low, v, preferred_element_type=jnp.float32)
        gq_all = jnp.dot(grad_scores, k, preferred_element_type=jnp.float32)
        att = att_all[:BLOCK]
        gq = gq_all[:BLOCK]
        for h in range(1, per_pair):
            att = jnp.where(heads[h], att_all[h * BLOCK : (h + 1) * BLOCK], att)
            gq = jnp.where(heads[h], gq_all[h * BLOCK : (h + 1) * BLOCK], gq)
        gk = lax.dot_general(grad_scores, qm, tn, preferred_element_type=jnp.float32)
        gv = lax.dot_general(probs_low, gm, tn, preferred_element_type=jnp.float32)
        att_ref[rows, :] = att.astype(att_ref.dtype)
        gq_ref[rows, :] = gq.astype(gq_ref.dtype)
        window = pl.ds(j * BLOCK, 3 * BLOCK)
        gwin_ref[0, window, :] += gk[: 3 * BLOCK]
        gwin_ref[1, window, :] += gv[: 3 * BLOCK]
        for r in range(RAND):
            there = pl.ds(picks[r], BLOCK)
            gpart_ref[r, 0, there, :] += gk[base + r * BLOCK : base + (r + 1) * BLOCK]
            gpart_ref[r, 1, there, :] += gv[base + r * BLOCK : base + (r + 1) * BLOCK]


def attend(meta, queries, grad_out, padded, glob, partners):
    tok_rows, width = queries.shape
    framed = padded.shape[1]
    pairs = width // LANES
    row_spec = pl.BlockSpec((tok_rows, LANES), lambda p, m: (0, p))
    win_spec = pl.BlockSpec((2, framed, LANES), lambda p, m: (0, 0, p))
    glob_spec = pl.BlockSpec((2, glob.shape[1], LANES), lambda p, m: (0, 0, p))
    part_spec = pl.BlockSpec((2, tok_rows, LANES), lambda p, m: (0, 0, p))
    out_specs = [
        row_spec,
        row_spec,
        win_spec,
        pl.BlockSpec((RAND, 2, tok_rows, LANES), lambda p, m: (0, 0, 0, p)),
    ]
    out_shape = [
        jax.ShapeDtypeStruct((tok_rows, width), jnp.bfloat16),
        jax.ShapeDtypeStruct((tok_rows, width), jnp.bfloat16),
        jax.ShapeDtypeStruct((2, framed, width), jnp.float32),
        jax.ShapeDtypeStruct((RAND, 2, tok_rows, width), jnp.float32),
    ]
    return pl.pallas_call(
        attend_kernel,
        grid_spec=pltpu.PrefetchScalarGridSpec(
            num_scalar_prefetch=1,
            grid=(pairs,),
            in_specs=[row_spec, row_spec, win_spec, glob_spec] + [part_spec] * RAND,
            out_specs=out_specs,
        ),
        out_shape=out_shape,
        compiler_params=pltpu.CompilerParams(dimension_semantics=("arbitrary",)),
    )(meta, queries, grad_out, padded, glob, *partners)


def local(queries, keys, values, grad_out, rand_blocks, global_ids):
    tok_rows, width = queries.shape
    block_count = tok_rows // BLOCK
    ctx_count = lax.axis_size("ctx")
    position = lax.axis_index("ctx")
    top_bit = ctx_count.bit_length() - 1
    block_iota = jnp.arange(block_count, dtype=jnp.int32)
    stacked = jnp.stack([keys, values])
    padded = padded_2(stacked, (("ctx", 1),), BLOCK)
    owners = global_ids // block_count
    local_ids = global_ids % block_count
    spread = [top_bit - 1 - matching for matching in range(RAND)]
    partners = [partner_2(stacked, "ctx", bit) for bit in spread]
    first_step = 1 << spread[0]
    candidates = []
    for global_slot in range(GLOBALS):
        start = local_ids[global_slot] * BLOCK
        own_piece = lax.dynamic_slice_in_dim(stacked, start, BLOCK, 1)
        far_piece = lax.dynamic_slice_in_dim(partners[0], start, BLOCK, 1)
        from_far = owners[global_slot] == (position ^ first_step)
        candidates.append(jnp.where(from_far, far_piece, own_piece))
    fetched = from_root(jnp.stack(candidates), "ctx", owners, first_step)
    glob = jnp.swapaxes(fetched, 0, 1).reshape(2, GLOBALS * BLOCK, width)
    global_block = position * block_count + block_iota
    seq_blocks = block_count * ctx_count
    meta = jnp.concatenate(
        [
            rand_blocks.reshape(-1).astype(jnp.int32),
            (global_block > 0).astype(jnp.int32),
            (global_block < seq_blocks - 1).astype(jnp.int32),
        ]
    )
    attended_out, grad_queries, gwin, gpart = attend(
        meta, queries, grad_out, padded, glob, partners
    )
    low = jnp.bfloat16
    from_right = passed_along(gwin[:, :BLOCK].astype(low), "ctx", -1).astype(jnp.float32)
    from_left = passed_along(gwin[:, -BLOCK:].astype(low), "ctx", 1).astype(jnp.float32)
    own_total = gwin[:, BLOCK:-BLOCK]
    own_total = own_total.at[:, tok_rows - BLOCK :].add(from_right)
    own_total = own_total.at[:, :BLOCK].add(from_left)
    for matching in range(RAND):
        own_total = own_total + partner_2(gpart[matching].astype(low), "ctx", spread[matching]).astype(
            jnp.float32
        )
    grad_keys = own_total[0].astype(jnp.bfloat16)
    grad_values = own_total[1].astype(jnp.bfloat16)
    return (attended_out, grad_queries, grad_keys, grad_values)


def solution(mesh):
    placed = (
        P(("dp", "ctx"), None),
        P(("dp", "ctx"), None),
        P(("dp", "ctx"), None),
        P(("dp", "ctx"), None),
        P(("dp", "ctx"), None),
        P("dp"),
    )
    return jax.shard_map(
        local,
        mesh=mesh,
        in_specs=placed,
        out_specs=(
            P(("dp", "ctx"), None),
            P(("dp", "ctx"), None),
            P(("dp", "ctx"), None),
            P(("dp", "ctx"), None),
        ),
        check_vma=False,
    )
```

```python
import jax
import jax.numpy as jnp
from jax import lax
from jax.sharding import PartitionSpec as P
from jax.experimental import pallas as pl
from jax.experimental.pallas import tpu as pltpu

HEAD_DIM = 64
BLOCK = 64
RAND = 3
GLOBALS = 2


SCORE_FLOOR = -1e30


def padded_2(array, sides, width):
    for axis, dim in sides:
        size, length = (lax.axis_size(axis), array.shape[dim])
        up = [(i, (i + 1) % size) for i in range(size - 1)]
        down = [(j, i) for i, j in up]
        last = lax.slice_in_dim(array, length - width, length, axis=dim)
        first = lax.slice_in_dim(array, 0, width, axis=dim)
        before = lax.ppermute(last, axis, up)
        after = lax.ppermute(first, axis, down)
        array = jnp.concatenate([before, array, after], axis=dim)
    return array


def from_root(blocks, axis, sources, mask):
    size = lax.axis_size(axis)
    position = lax.axis_index(axis)
    shape = (-1,) + (1,) * (blocks.ndim - 2)
    core = position % 2
    sibling = [(i, i ^ 1) for i in range(size)]

    def holds(partner):
        return (((sources ^ partner) & ~mask) == 0).reshape(shape)

    mine = jnp.where(core == 0, blocks[:, 0], blocks[:, 1])
    theirs = jnp.where(core == 0, blocks[:, 1], blocks[:, 0])
    received = lax.ppermute(theirs, axis, sibling)
    carried = jnp.where(holds(position ^ 1), received, mine)
    mask = mask | 1
    for level in range(1, size.bit_length() - 1):
        step = 1 << level
        if mask & step:
            continue
        received = lax.ppermute(carried, axis, [(i, i ^ step) for i in range(size)])
        carried = jnp.where(holds(position ^ step), received, carried)
        mask = mask | step
    other = lax.ppermute(carried, axis, sibling)
    first = jnp.where(core == 0, carried, other)
    second = jnp.where(core == 0, other, carried)
    return jnp.stack([first, second], axis=1)


def partner_2(array, axis, distance):
    return lax.ppermute(array, axis, [(i, i ^ 1 << distance) for i in range(lax.axis_size(axis))])


def passed_along(array, axis, by):
    size = lax.axis_size(axis)
    pairs = [(i, i + by) for i in range(size) if 0 <= i + by < size]
    return lax.ppermute(array, axis, pairs)


LANES = 128


def attend_kernel(meta_ref, q_ref, g_ref, win_ref, glob_ref, *rest):
    partner_refs = rest[:RAND]
    att_ref, gq_ref, gwin_ref, gpart_ref = rest[RAND:]
    block_count = q_ref.shape[0] // BLOCK
    listed = 3 + GLOBALS + RAND
    scale_factor = HEAD_DIM ** (-0.5)
    gwin_ref[...] = jnp.zeros_like(gwin_ref)
    gpart_ref[...] = jnp.zeros_like(gpart_ref)
    lane = lax.broadcasted_iota(jnp.int32, (BLOCK, LANES), 1)
    per_pair = LANES // HEAD_DIM
    col = lax.broadcasted_iota(jnp.int32, (per_pair * BLOCK, listed * BLOCK), 1)
    nt = (((1,), (1,)), ((), ()))
    tn = (((0,), (0,)), ((), ()))
    base = (3 + GLOBALS) * BLOCK
    for j in range(block_count):
        rows = pl.ds(j * BLOCK, BLOCK)
        q = q_ref[rows, :]
        g = g_ref[rows, :]
        picks = [pl.multiple_of(meta_ref[j * RAND + r] * BLOCK, BLOCK) for r in range(RAND)]
        left_ok = meta_ref[block_count * RAND + j]
        right_ok = meta_ref[block_count * RAND + block_count + j]

        def gather(kv):
            parts = [win_ref[kv, pl.ds(j * BLOCK, 3 * BLOCK), :], glob_ref[kv]]
            for r in range(RAND):
                parts.append(partner_refs[r][kv, pl.ds(picks[r], BLOCK), :])
            return jnp.concatenate(parts, axis=0)

        k = gather(0)
        v = gather(1)
        invalid = ((col < BLOCK) & (left_ok == 0)) | (
            (col >= 2 * BLOCK) & (col < 3 * BLOCK) & (right_ok == 0)
        )
        heads = [(lane >= h * HEAD_DIM) & (lane < (h + 1) * HEAD_DIM) for h in range(per_pair)]
        qm = jnp.concatenate([jnp.where(m, q, jnp.zeros_like(q)) for m in heads], axis=0)
        gm = jnp.concatenate([jnp.where(m, g, jnp.zeros_like(g)) for m in heads], axis=0)
        scores = lax.dot_general(qm, k, nt, preferred_element_type=jnp.float32) * scale_factor
        scores = jnp.where(invalid, SCORE_FLOOR, scores)
        highest = jnp.max(scores, axis=-1, keepdims=True)
        raw_weights = jnp.exp(scores - highest)
        weight_total = jnp.sum(raw_weights, axis=-1, keepdims=True)
        probs = raw_weights / weight_total
        probs_low = probs.astype(jnp.bfloat16)
        grad_probs = lax.dot_general(gm, v, nt, preferred_element_type=jnp.float32)
        inner = jnp.sum(probs * grad_probs, axis=-1, keepdims=True)
        grad_scores = (scale_factor * probs * (grad_probs - inner)).astype(jnp.bfloat16)
        att_all = jnp.dot(probs_low, v, preferred_element_type=jnp.float32)
        gq_all = jnp.dot(grad_scores, k, preferred_element_type=jnp.float32)
        att = att_all[:BLOCK]
        gq = gq_all[:BLOCK]
        for h in range(1, per_pair):
            att = jnp.where(heads[h], att_all[h * BLOCK : (h + 1) * BLOCK], att)
            gq = jnp.where(heads[h], gq_all[h * BLOCK : (h + 1) * BLOCK], gq)
        gk = lax.dot_general(grad_scores, qm, tn, preferred_element_type=jnp.float32)
        gv = lax.dot_general(probs_low, gm, tn, preferred_element_type=jnp.float32)
        att_ref[rows, :] = att.astype(att_ref.dtype)
        gq_ref[rows, :] = gq.astype(gq_ref.dtype)
        window = pl.ds(j * BLOCK, 3 * BLOCK)
        gwin_ref[0, window, :] += gk[: 3 * BLOCK]
        gwin_ref[1, window, :] += gv[: 3 * BLOCK]
        for r in range(RAND):
            there = pl.ds(picks[r], BLOCK)
            gpart_ref[r, 0, there, :] += gk[base + r * BLOCK : base + (r + 1) * BLOCK]
            gpart_ref[r, 1, there, :] += gv[base + r * BLOCK : base + (r + 1) * BLOCK]


def attend(meta, queries, grad_out, padded, glob, partners):
    tok_rows, width = queries.shape
    framed = padded.shape[1]
    pairs = width // LANES
    row_spec = pl.BlockSpec((tok_rows, LANES), lambda p, m: (0, p))
    win_spec = pl.BlockSpec((2, framed, LANES), lambda p, m: (0, 0, p))
    glob_spec = pl.BlockSpec((2, glob.shape[1], LANES), lambda p, m: (0, 0, p))
    part_spec = pl.BlockSpec((2, tok_rows, LANES), lambda p, m: (0, 0, p))
    out_specs = [
        row_spec,
        row_spec,
        win_spec,
        pl.BlockSpec((RAND, 2, tok_rows, LANES), lambda p, m: (0, 0, 0, p)),
    ]
    out_shape = [
        jax.ShapeDtypeStruct((tok_rows, width), jnp.bfloat16),
        jax.ShapeDtypeStruct((tok_rows, width), jnp.bfloat16),
        jax.ShapeDtypeStruct((2, framed, width), jnp.float32),
        jax.ShapeDtypeStruct((RAND, 2, tok_rows, width), jnp.float32),
    ]
    return pl.pallas_call(
        attend_kernel,
        grid_spec=pltpu.PrefetchScalarGridSpec(
            num_scalar_prefetch=1,
            grid=(pairs,),
            in_specs=[row_spec, row_spec, win_spec, glob_spec] + [part_spec] * RAND,
            out_specs=out_specs,
        ),
        out_shape=out_shape,
        compiler_params=pltpu.CompilerParams(dimension_semantics=("arbitrary",)),
    )(meta, queries, grad_out, padded, glob, *partners)


def local_body(queries, keys, values, grad_out, rand_blocks, global_ids):
    tok_rows, width = queries.shape
    block_count = tok_rows // BLOCK
    ctx_count = lax.axis_size("ctx")
    position = lax.axis_index("ctx")
    top_bit = ctx_count.bit_length() - 1
    block_iota = jnp.arange(block_count, dtype=jnp.int32)
    stacked = jnp.stack([keys, values])
    padded = padded_2(stacked, (("ctx", 1),), BLOCK)
    owners = global_ids // block_count
    local_ids = global_ids % block_count
    spread = [top_bit - 1 - matching for matching in range(RAND)]
    partners = []
    for bit in spread:
        partners.append(partner_2(stacked, "ctx", bit))
    first_step = 1 << spread[0]
    candidates = []
    for global_slot in range(GLOBALS):
        start = local_ids[global_slot] * BLOCK
        own_piece = lax.dynamic_slice_in_dim(stacked, start, BLOCK, 1)
        far_piece = lax.dynamic_slice_in_dim(partners[0], start, BLOCK, 1)
        from_far = owners[global_slot] == (position ^ first_step)
        candidates.append(jnp.where(from_far, far_piece, own_piece))
    fetched = from_root(jnp.stack(candidates), "ctx", owners, first_step)
    glob = jnp.swapaxes(fetched, 0, 1).reshape(2, GLOBALS * BLOCK, width)
    global_block = position * block_count + block_iota
    seq_blocks = block_count * ctx_count
    meta = jnp.concatenate(
        [
            rand_blocks.reshape(-1).astype(jnp.int32),
            (global_block > 0).astype(jnp.int32),
            (global_block < seq_blocks - 1).astype(jnp.int32),
        ]
    )
    attended_out, grad_queries, gwin, gpart = attend(
        meta, queries, grad_out, padded, glob, partners
    )
    low = jnp.bfloat16
    from_right = passed_along(gwin[:, :BLOCK].astype(low), "ctx", -1).astype(jnp.float32)
    from_left = passed_along(gwin[:, -BLOCK:].astype(low), "ctx", 1).astype(jnp.float32)
    own_total = gwin[:, BLOCK:-BLOCK]
    own_total = own_total.at[:, tok_rows - BLOCK :].add(from_right)
    own_total = own_total.at[:, :BLOCK].add(from_left)
    for matching in range(RAND):
        own_total = own_total + partner_2(gpart[matching].astype(low), "ctx", spread[matching]).astype(
            jnp.float32
        )
    grad_keys = own_total[0].astype(jnp.bfloat16)
    grad_values = own_total[1].astype(jnp.bfloat16)
    return (attended_out, grad_queries, grad_keys, grad_values)


def solution(mesh):
    placed = (
        P(("dp", "ctx"), None),
        P(("dp", "ctx"), None),
        P(("dp", "ctx"), None),
        P(("dp", "ctx"), None),
        P(("dp", "ctx"), None),
        P("dp"),
    )
    return jax.shard_map(
        local_body,
        mesh=mesh,
        in_specs=placed,
        out_specs=(
            P(("dp", "ctx"), None),
            P(("dp", "ctx"), None),
            P(("dp", "ctx"), None),
            P(("dp", "ctx"), None),
        ),
        check_vma=False,
    )
```

```python
import jax
import jax.numpy as jnp
from jax import lax
from jax.sharding import PartitionSpec as P
from jax.experimental import pallas as pl
from jax.experimental.pallas import tpu as pltpu

HEAD_DIM = 64
BLOCK = 64
RAND = 3
GLOBALS = 2


SCORE_FLOOR = -1e30


def padded_2(array, sides, width):
    for axis, dim in sides:
        size, length = (lax.axis_size(axis), array.shape[dim])
        up = [(i, (i + 1) % size) for i in range(size - 1)]
        down = [(j, i) for i, j in up]
        last = lax.slice_in_dim(array, length - width, length, axis=dim)
        first = lax.slice_in_dim(array, 0, width, axis=dim)
        before = lax.ppermute(last, axis, up)
        after = lax.ppermute(first, axis, down)
        array = jnp.concatenate([before, array, after], axis=dim)
    return array


def from_root(blocks, axis, sources, mask):
    size = lax.axis_size(axis)
    position = lax.axis_index(axis)
    shape = (-1,) + (1,) * (blocks.ndim - 2)
    core = position % 2
    sibling = [(i, i ^ 1) for i in range(size)]

    def holds(partner):
        return (((sources ^ partner) & ~mask) == 0).reshape(shape)

    mine = jnp.where(core == 0, blocks[:, 0], blocks[:, 1])
    theirs = jnp.where(core == 0, blocks[:, 1], blocks[:, 0])
    received = lax.ppermute(theirs, axis, sibling)
    carried = jnp.where(holds(position ^ 1), received, mine)
    mask = mask | 1
    for level in range(1, size.bit_length() - 1):
        step = 1 << level
        if mask & step:
            continue
        received = lax.ppermute(carried, axis, [(i, i ^ step) for i in range(size)])
        carried = jnp.where(holds(position ^ step), received, carried)
        mask = mask | step
    other = lax.ppermute(carried, axis, sibling)
    first = jnp.where(core == 0, carried, other)
    second = jnp.where(core == 0, other, carried)
    return jnp.stack([first, second], axis=1)


def partner_2(array, axis, distance):
    return lax.ppermute(array, axis, [(i, i ^ 1 << distance) for i in range(lax.axis_size(axis))])


def passed_along(array, axis, by):
    size = lax.axis_size(axis)
    pairs = [(i, i + by) for i in range(size) if 0 <= i + by < size]
    return lax.ppermute(array, axis, pairs)


LANES = 128


def attend_kernel(meta_ref, q_ref, g_ref, win_ref, glob_ref, *rest):
    partner_refs = rest[:RAND]
    att_ref, gq_ref, gwin_ref, gpart_ref = rest[RAND:]
    block_count = q_ref.shape[0] // BLOCK
    listed = 3 + GLOBALS + RAND
    scale_factor = HEAD_DIM ** (-0.5)
    gwin_ref[...] = jnp.zeros_like(gwin_ref)
    gpart_ref[...] = jnp.zeros_like(gpart_ref)
    lane = lax.broadcasted_iota(jnp.int32, (BLOCK, LANES), 1)
    per_pair = LANES // HEAD_DIM
    col = lax.broadcasted_iota(jnp.int32, (per_pair * BLOCK, listed * BLOCK), 1)
    nt = (((1,), (1,)), ((), ()))
    tn = (((0,), (0,)), ((), ()))
    base = (3 + GLOBALS) * BLOCK
    for j in range(block_count):
        rows = pl.ds(j * BLOCK, BLOCK)
        q = q_ref[rows, :]
        g = g_ref[rows, :]
        picks = [pl.multiple_of(meta_ref[j * RAND + r] * BLOCK, BLOCK) for r in range(RAND)]
        left_ok = meta_ref[block_count * RAND + j]
        right_ok = meta_ref[block_count * RAND + block_count + j]

        def gather(kv):
            parts = [win_ref[kv, pl.ds(j * BLOCK, 3 * BLOCK), :], glob_ref[kv]]
            for r in range(RAND):
                parts.append(partner_refs[r][kv, pl.ds(picks[r], BLOCK), :])
            return jnp.concatenate(parts, axis=0)

        k = gather(0)
        v = gather(1)
        invalid = ((col < BLOCK) & (left_ok == 0)) | (
            (col >= 2 * BLOCK) & (col < 3 * BLOCK) & (right_ok == 0)
        )
        heads = [(lane >= h * HEAD_DIM) & (lane < (h + 1) * HEAD_DIM) for h in range(per_pair)]
        qm = jnp.concatenate([jnp.where(m, q, jnp.zeros_like(q)) for m in heads], axis=0)
        gm = jnp.concatenate([jnp.where(m, g, jnp.zeros_like(g)) for m in heads], axis=0)
        scores = lax.dot_general(qm, k, nt, preferred_element_type=jnp.float32) * scale_factor
        scores = jnp.where(invalid, SCORE_FLOOR, scores)
        highest = jnp.max(scores, axis=-1, keepdims=True)
        raw_weights = jnp.exp(scores - highest)
        weight_total = jnp.sum(raw_weights, axis=-1, keepdims=True)
        probs = raw_weights / weight_total
        probs_low = probs.astype(jnp.bfloat16)
        grad_probs = lax.dot_general(gm, v, nt, preferred_element_type=jnp.float32)
        inner = jnp.sum(probs * grad_probs, axis=-1, keepdims=True)
        grad_scores = (scale_factor * probs * (grad_probs - inner)).astype(jnp.bfloat16)
        att_all = jnp.dot(probs_low, v, preferred_element_type=jnp.float32)
        gq_all = jnp.dot(grad_scores, k, preferred_element_type=jnp.float32)
        att = att_all[:BLOCK]
        gq = gq_all[:BLOCK]
        for h in range(1, per_pair):
            att = jnp.where(heads[h], att_all[h * BLOCK : (h + 1) * BLOCK], att)
            gq = jnp.where(heads[h], gq_all[h * BLOCK : (h + 1) * BLOCK], gq)
        gk = lax.dot_general(grad_scores, qm, tn, preferred_element_type=jnp.float32)
        gv = lax.dot_general(probs_low, gm, tn, preferred_element_type=jnp.float32)
        att_ref[rows, :] = att.astype(att_ref.dtype)
        gq_ref[rows, :] = gq.astype(gq_ref.dtype)
        window = pl.ds(j * BLOCK, 3 * BLOCK)
        gwin_ref[0, window, :] += gk[: 3 * BLOCK]
        gwin_ref[1, window, :] += gv[: 3 * BLOCK]
        for r in range(RAND):
            there = pl.ds(picks[r], BLOCK)
            gpart_ref[r, 0, there, :] += gk[base + r * BLOCK : base + (r + 1) * BLOCK]
            gpart_ref[r, 1, there, :] += gv[base + r * BLOCK : base + (r + 1) * BLOCK]


def attend(meta, queries, grad_out, padded, glob, partners):
    tok_rows, width = queries.shape
    framed = padded.shape[1]
    pairs = width // LANES
    row_spec = pl.BlockSpec((tok_rows, LANES), lambda p, m: (0, p))
    win_spec = pl.BlockSpec((2, framed, LANES), lambda p, m: (0, 0, p))
    glob_spec = pl.BlockSpec((2, glob.shape[1], LANES), lambda p, m: (0, 0, p))
    part_spec = pl.BlockSpec((2, tok_rows, LANES), lambda p, m: (0, 0, p))
    out_specs = [
        row_spec,
        row_spec,
        win_spec,
        pl.BlockSpec((RAND, 2, tok_rows, LANES), lambda p, m: (0, 0, 0, p)),
    ]
    out_shape = [
        jax.ShapeDtypeStruct((tok_rows, width), jnp.bfloat16),
        jax.ShapeDtypeStruct((tok_rows, width), jnp.bfloat16),
        jax.ShapeDtypeStruct((2, framed, width), jnp.float32),
        jax.ShapeDtypeStruct((RAND, 2, tok_rows, width), jnp.float32),
    ]
    return pl.pallas_call(
        attend_kernel,
        grid_spec=pltpu.PrefetchScalarGridSpec(
            num_scalar_prefetch=1,
            grid=(pairs,),
            in_specs=[row_spec, row_spec, win_spec, glob_spec] + [part_spec] * RAND,
            out_specs=out_specs,
        ),
        out_shape=out_shape,
        compiler_params=pltpu.CompilerParams(dimension_semantics=("arbitrary",)),
    )(meta, queries, grad_out, padded, glob, *partners)


def local_body(queries, keys, values, grad_out, rand_blocks, global_ids):
    tok_rows, width = queries.shape
    block_count = tok_rows // BLOCK
    ctx_count = lax.axis_size("ctx")
    position = lax.axis_index("ctx")
    top_bit = ctx_count.bit_length() - 1
    block_iota = jnp.arange(block_count, dtype=jnp.int32)
    stacked = jnp.stack([keys, values])
    padded = padded_2(stacked, (("ctx", 1),), BLOCK)
    owners = global_ids // block_count
    local_ids = global_ids % block_count
    spread = [top_bit - 1 - matching for matching in range(RAND)]
    partners = []
    for bit in spread:
        partners.append(partner_2(stacked, "ctx", bit))
    candidates = [
        lax.dynamic_slice_in_dim(stacked, local_ids[global_slot] * BLOCK, BLOCK, 1)
        for global_slot in range(GLOBALS)
    ]
    fetched = from_root(jnp.stack(candidates), "ctx", owners, 0)
    glob = jnp.swapaxes(fetched, 0, 1).reshape(2, GLOBALS * BLOCK, width)
    global_block = position * block_count + block_iota
    seq_blocks = block_count * ctx_count
    meta = jnp.concatenate(
        [
            rand_blocks.reshape(-1).astype(jnp.int32),
            (global_block > 0).astype(jnp.int32),
            (global_block < seq_blocks - 1).astype(jnp.int32),
        ]
    )
    attended_out, grad_queries, gwin, gpart = attend(
        meta, queries, grad_out, padded, glob, partners
    )
    low = jnp.bfloat16
    from_right = passed_along(gwin[:, :BLOCK].astype(low), "ctx", -1).astype(jnp.float32)
    from_left = passed_along(gwin[:, -BLOCK:].astype(low), "ctx", 1).astype(jnp.float32)
    own_total = gwin[:, BLOCK:-BLOCK]
    own_total = own_total.at[:, tok_rows - BLOCK :].add(from_right)
    own_total = own_total.at[:, :BLOCK].add(from_left)
    for matching in range(RAND):
        own_total = own_total + partner_2(gpart[matching].astype(low), "ctx", spread[matching]).astype(
            jnp.float32
        )
    grad_keys = own_total[0].astype(jnp.bfloat16)
    grad_values = own_total[1].astype(jnp.bfloat16)
    return (attended_out, grad_queries, grad_keys, grad_values)


def solution(mesh):
    placed = (
        P(("dp", "ctx"), None),
        P(("dp", "ctx"), None),
        P(("dp", "ctx"), None),
        P(("dp", "ctx"), None),
        P(("dp", "ctx"), None),
        P("dp"),
    )
    return jax.shard_map(
        local_body,
        mesh=mesh,
        in_specs=placed,
        out_specs=(
            P(("dp", "ctx"), None),
            P(("dp", "ctx"), None),
            P(("dp", "ctx"), None),
            P(("dp", "ctx"), None),
        ),
        check_vma=False,
    )
```

```python
import jax
import jax.numpy as jnp
from jax import lax
from jax.sharding import PartitionSpec as P
from jax.experimental import pallas as pl
from jax.experimental.pallas import tpu as pltpu

HEAD_DIM = 64
BLOCK = 64
RAND = 3
GLOBALS = 2


SCORE_FLOOR = -1e30


def padded_2(array, sides, width):
    for axis, dim in sides:
        size, length = (lax.axis_size(axis), array.shape[dim])
        up = [(i, (i + 1) % size) for i in range(size - 1)]
        down = [(j, i) for i, j in up]
        last = lax.slice_in_dim(array, length - width, length, axis=dim)
        first = lax.slice_in_dim(array, 0, width, axis=dim)
        before = lax.ppermute(last, axis, up)
        after = lax.ppermute(first, axis, down)
        array = jnp.concatenate([before, array, after], axis=dim)
    return array


def from_root(blocks, axis, sources, mask):
    size = lax.axis_size(axis)
    position = lax.axis_index(axis)
    shape = (-1,) + (1,) * (blocks.ndim - 2)
    core = position % 2
    sibling = [(i, i ^ 1) for i in range(size)]

    def holds(partner):
        return (((sources ^ partner) & ~mask) == 0).reshape(shape)

    mine = jnp.where(core == 0, blocks[:, 0], blocks[:, 1])
    theirs = jnp.where(core == 0, blocks[:, 1], blocks[:, 0])
    received = lax.ppermute(theirs, axis, sibling)
    carried = jnp.where(holds(position ^ 1), received, mine)
    mask = mask | 1
    for level in range(1, size.bit_length() - 1):
        step = 1 << level
        if mask & step:
            continue
        received = lax.ppermute(carried, axis, [(i, i ^ step) for i in range(size)])
        carried = jnp.where(holds(position ^ step), received, carried)
        mask = mask | step
    other = lax.ppermute(carried, axis, sibling)
    first = jnp.where(core == 0, carried, other)
    second = jnp.where(core == 0, other, carried)
    return jnp.stack([first, second], axis=1)


def partner_2(array, axis, distance):
    return lax.ppermute(array, axis, [(i, i ^ 1 << distance) for i in range(lax.axis_size(axis))])


def passed_along(array, axis, by):
    size = lax.axis_size(axis)
    pairs = [(i, i + by) for i in range(size) if 0 <= i + by < size]
    return lax.ppermute(array, axis, pairs)


LANES = 128


def attend_kernel(meta_ref, q_ref, g_ref, win_ref, glob_ref, *rest):
    partner_refs = rest[:RAND]
    att_ref, gq_ref, gwin_ref, gpart_ref, stats_ref = rest[RAND:]
    block_count = q_ref.shape[0] // BLOCK
    listed = 3 + GLOBALS + RAND
    scale_factor = HEAD_DIM ** (-0.5)
    gwin_ref[...] = jnp.zeros_like(gwin_ref)
    gpart_ref[...] = jnp.zeros_like(gpart_ref)
    lane = lax.broadcasted_iota(jnp.int32, (BLOCK, LANES), 1)
    per_pair = LANES // HEAD_DIM
    col = lax.broadcasted_iota(jnp.int32, (per_pair * BLOCK, listed * BLOCK), 1)
    nt = (((1,), (1,)), ((), ()))
    tn = (((0,), (0,)), ((), ()))
    base = (3 + GLOBALS) * BLOCK
    for j in range(block_count):
        rows = pl.ds(j * BLOCK, BLOCK)
        q = q_ref[rows, :]
        g = g_ref[rows, :]
        picks = [pl.multiple_of(meta_ref[j * RAND + r] * BLOCK, BLOCK) for r in range(RAND)]
        left_ok = meta_ref[block_count * RAND + j]
        right_ok = meta_ref[block_count * RAND + block_count + j]

        def gather(kv):
            parts = [win_ref[kv, pl.ds(j * BLOCK, 3 * BLOCK), :], glob_ref[kv]]
            for r in range(RAND):
                parts.append(partner_refs[r][kv, pl.ds(picks[r], BLOCK), :])
            return jnp.concatenate(parts, axis=0)

        k = gather(0)
        v = gather(1)
        invalid = ((col < BLOCK) & (left_ok == 0)) | (
            (col >= 2 * BLOCK) & (col < 3 * BLOCK) & (right_ok == 0)
        )
        heads = [(lane >= h * HEAD_DIM) & (lane < (h + 1) * HEAD_DIM) for h in range(per_pair)]
        qm = jnp.concatenate([jnp.where(m, q, jnp.zeros_like(q)) for m in heads], axis=0)
        gm = jnp.concatenate([jnp.where(m, g, jnp.zeros_like(g)) for m in heads], axis=0)
        scores = lax.dot_general(qm, k, nt, preferred_element_type=jnp.float32) * scale_factor
        scores = jnp.where(invalid, SCORE_FLOOR, scores)
        highest = jnp.max(scores, axis=-1, keepdims=True)
        raw_weights = jnp.exp(scores - highest)
        weight_total = jnp.sum(raw_weights, axis=-1, keepdims=True)
        probs = raw_weights / weight_total
        probs_low = probs.astype(jnp.bfloat16)
        grad_probs = lax.dot_general(gm, v, nt, preferred_element_type=jnp.float32)
        inner = jnp.sum(probs * grad_probs, axis=-1, keepdims=True)
        grad_scores = (scale_factor * probs * (grad_probs - inner)).astype(jnp.bfloat16)
        att_all = jnp.dot(probs_low, v, preferred_element_type=jnp.float32)
        gq_all = jnp.dot(grad_scores, k, preferred_element_type=jnp.float32)
        att = att_all[:BLOCK]
        gq = gq_all[:BLOCK]
        for h in range(1, per_pair):
            att = jnp.where(heads[h], att_all[h * BLOCK : (h + 1) * BLOCK], att)
            gq = jnp.where(heads[h], gq_all[h * BLOCK : (h + 1) * BLOCK], gq)
        gk = lax.dot_general(grad_scores, qm, tn, preferred_element_type=jnp.float32)
        gv = lax.dot_general(probs_low, gm, tn, preferred_element_type=jnp.float32)
        stacked_rows = per_pair * BLOCK
        for t, stat in enumerate((highest, weight_total, inner)):
            stats_ref[0, pl.ds((j * 3 + t) * stacked_rows, stacked_rows), :] = jnp.broadcast_to(
                stat, (stacked_rows, LANES)
            )
        att_ref[rows, :] = att.astype(att_ref.dtype)
        gq_ref[rows, :] = gq.astype(gq_ref.dtype)
        window = pl.ds(j * BLOCK, 3 * BLOCK)
        gwin_ref[0, window, :] += gk[: 3 * BLOCK]
        gwin_ref[1, window, :] += gv[: 3 * BLOCK]
        for r in range(RAND):
            there = pl.ds(picks[r], BLOCK)
            gpart_ref[r, 0, there, :] += gk[base + r * BLOCK : base + (r + 1) * BLOCK]
            gpart_ref[r, 1, there, :] += gv[base + r * BLOCK : base + (r + 1) * BLOCK]


def attend(meta, queries, grad_out, padded, glob, partners):
    tok_rows, width = queries.shape
    framed = padded.shape[1]
    pairs = width // LANES
    stat_rows = 3 * tok_rows * (LANES // HEAD_DIM)
    row_spec = pl.BlockSpec((tok_rows, LANES), lambda p, m: (0, p))
    win_spec = pl.BlockSpec((2, framed, LANES), lambda p, m: (0, 0, p))
    glob_spec = pl.BlockSpec((2, glob.shape[1], LANES), lambda p, m: (0, 0, p))
    part_spec = pl.BlockSpec((2, tok_rows, LANES), lambda p, m: (0, 0, p))
    out_specs = [
        row_spec,
        row_spec,
        win_spec,
        pl.BlockSpec((RAND, 2, tok_rows, LANES), lambda p, m: (0, 0, 0, p)),
        pl.BlockSpec((1, stat_rows, LANES), lambda p, m: (p, 0, 0)),
    ]
    out_shape = [
        jax.ShapeDtypeStruct((tok_rows, width), jnp.bfloat16),
        jax.ShapeDtypeStruct((tok_rows, width), jnp.bfloat16),
        jax.ShapeDtypeStruct((2, framed, width), jnp.float32),
        jax.ShapeDtypeStruct((RAND, 2, tok_rows, width), jnp.float32),
        jax.ShapeDtypeStruct((pairs, stat_rows, LANES), jnp.float32),
    ]
    return pl.pallas_call(
        attend_kernel,
        grid_spec=pltpu.PrefetchScalarGridSpec(
            num_scalar_prefetch=1,
            grid=(pairs,),
            in_specs=[row_spec, row_spec, win_spec, glob_spec] + [part_spec] * RAND,
            out_specs=out_specs,
        ),
        out_shape=out_shape,
        compiler_params=pltpu.CompilerParams(dimension_semantics=("arbitrary",)),
    )(meta, queries, grad_out, padded, glob, *partners)


def partner_kernel(pick_ref, qd_ref, st_ref, kv_ref, out_ref):
    block_count = qd_ref.shape[1] // BLOCK
    per_pair = LANES // HEAD_DIM
    stacked_rows = per_pair * BLOCK
    scale_factor = HEAD_DIM ** (-0.5)
    nt = (((1,), (1,)), ((), ()))
    tn = (((0,), (0,)), ((), ()))
    out_ref[...] = jnp.zeros_like(out_ref)
    lane = lax.broadcasted_iota(jnp.int32, (BLOCK, LANES), 1)
    heads = [(lane >= h * HEAD_DIM) & (lane < (h + 1) * HEAD_DIM) for h in range(per_pair)]
    for j in range(block_count):
        rows = pl.ds(j * BLOCK, BLOCK)
        q = qd_ref[0, rows, :]
        g = qd_ref[1, rows, :]
        qm = jnp.concatenate([jnp.where(m, q, jnp.zeros_like(q)) for m in heads], axis=0)
        gm = jnp.concatenate([jnp.where(m, g, jnp.zeros_like(g)) for m in heads], axis=0)
        pick = pl.ds(pl.multiple_of(pick_ref[j] * BLOCK, BLOCK), BLOCK)
        k = kv_ref[0, pick, :]
        v = kv_ref[1, pick, :]
        highest, weight_total, inner = (
            st_ref[0, pl.ds((j * 3 + t) * stacked_rows, stacked_rows), :][:, :BLOCK]
            for t in range(3)
        )
        scores = lax.dot_general(qm, k, nt, preferred_element_type=jnp.float32) * scale_factor
        probs = jnp.exp(scores - highest) / weight_total
        probs_low = probs.astype(jnp.bfloat16)
        grad_probs = lax.dot_general(gm, v, nt, preferred_element_type=jnp.float32)
        grad_scores = (scale_factor * probs * (grad_probs - inner)).astype(jnp.bfloat16)
        out_ref[0, pick, :] += lax.dot_general(grad_scores, qm, tn, preferred_element_type=jnp.float32)
        out_ref[1, pick, :] += lax.dot_general(probs_low, gm, tn, preferred_element_type=jnp.float32)


def partner_terms(picks, qd, stats, stacked):
    _, tok_rows, width = stacked.shape
    pairs, stat_rows, _ = stats.shape
    slab_spec = pl.BlockSpec((2, tok_rows, LANES), lambda p, m: (0, 0, p))
    return pl.pallas_call(
        partner_kernel,
        grid_spec=pltpu.PrefetchScalarGridSpec(
            num_scalar_prefetch=1,
            grid=(pairs,),
            in_specs=[slab_spec, pl.BlockSpec((1, stat_rows, LANES), lambda p, m: (p, 0, 0)), slab_spec],
            out_specs=slab_spec,
        ),
        out_shape=jax.ShapeDtypeStruct((2, tok_rows, width), jnp.float32),
        compiler_params=pltpu.CompilerParams(dimension_semantics=("arbitrary",)),
    )(picks, qd, stats, stacked)


def local_body(queries, keys, values, grad_out, rand_blocks, global_ids):
    tok_rows, width = queries.shape
    block_count = tok_rows // BLOCK
    ctx_count = lax.axis_size("ctx")
    position = lax.axis_index("ctx")
    top_bit = ctx_count.bit_length() - 1
    block_iota = jnp.arange(block_count, dtype=jnp.int32)
    stacked = jnp.stack([keys, values])
    padded = padded_2(stacked, (("ctx", 1),), BLOCK)
    owners = global_ids // block_count
    local_ids = global_ids % block_count
    spread = [top_bit - 1 - matching for matching in range(RAND)]
    partners = []
    for matching, bit in enumerate(spread):
        partners.append(partner_2(stacked, "ctx", bit))
        if matching == 0:
            far_qd = partner_2(jnp.stack([queries, grad_out]), "ctx", bit)
            far_picks = partner_2(rand_blocks[:, 0].astype(jnp.float32), "ctx", bit)
    candidates = [
        lax.dynamic_slice_in_dim(stacked, local_ids[global_slot] * BLOCK, BLOCK, 1)
        for global_slot in range(GLOBALS)
    ]
    fetched = from_root(jnp.stack(candidates), "ctx", owners, 0)
    glob = jnp.swapaxes(fetched, 0, 1).reshape(2, GLOBALS * BLOCK, width)
    global_block = position * block_count + block_iota
    seq_blocks = block_count * ctx_count
    meta = jnp.concatenate(
        [
            rand_blocks.reshape(-1).astype(jnp.int32),
            (global_block > 0).astype(jnp.int32),
            (global_block < seq_blocks - 1).astype(jnp.int32),
        ]
    )
    attended_out, grad_queries, gwin, gpart, stats = attend(
        meta, queries, grad_out, padded, glob, partners
    )
    low = jnp.bfloat16
    from_right = passed_along(gwin[:, :BLOCK].astype(low), "ctx", -1).astype(jnp.float32)
    from_left = passed_along(gwin[:, -BLOCK:].astype(low), "ctx", 1).astype(jnp.float32)
    own_total = gwin[:, BLOCK:-BLOCK]
    own_total = own_total.at[:, tok_rows - BLOCK :].add(from_right)
    own_total = own_total.at[:, :BLOCK].add(from_left)
    for matching in range(1, RAND):
        own_total = own_total + partner_2(gpart[matching].astype(low), "ctx", spread[matching]).astype(
            jnp.float32
        )
    far_stats = partner_2(stats[:, :, 0], "ctx", spread[0])
    far_stats = jnp.broadcast_to(far_stats[:, :, None], stats.shape)
    own_total = own_total + partner_terms(far_picks.astype(jnp.int32), far_qd, far_stats, stacked)
    grad_keys = own_total[0].astype(jnp.bfloat16)
    grad_values = own_total[1].astype(jnp.bfloat16)
    return (attended_out, grad_queries, grad_keys, grad_values)


def solution(mesh):
    placed = (
        P(("dp", "ctx"), None),
        P(("dp", "ctx"), None),
        P(("dp", "ctx"), None),
        P(("dp", "ctx"), None),
        P(("dp", "ctx"), None),
        P("dp"),
    )
    return jax.shard_map(
        local_body,
        mesh=mesh,
        in_specs=placed,
        out_specs=(
            P(("dp", "ctx"), None),
            P(("dp", "ctx"), None),
            P(("dp", "ctx"), None),
            P(("dp", "ctx"), None),
        ),
        check_vma=False,
    )
```

```python
import jax
import jax.numpy as jnp
from jax import lax
from jax.sharding import PartitionSpec as P
from jax.experimental import pallas as pl
from jax.experimental.pallas import tpu as pltpu

HEAD_DIM = 64
BLOCK = 64
RAND = 3
GLOBALS = 2


SCORE_FLOOR = -1e30


def padded_2(array, sides, width):
    for axis, dim in sides:
        size, length = (lax.axis_size(axis), array.shape[dim])
        up = [(i, (i + 1) % size) for i in range(size - 1)]
        down = [(j, i) for i, j in up]
        last = lax.slice_in_dim(array, length - width, length, axis=dim)
        first = lax.slice_in_dim(array, 0, width, axis=dim)
        before = lax.ppermute(last, axis, up)
        after = lax.ppermute(first, axis, down)
        array = jnp.concatenate([before, array, after], axis=dim)
    return array


def from_root(blocks, axis, sources, mask):
    size = lax.axis_size(axis)
    position = lax.axis_index(axis)
    shape = (-1,) + (1,) * (blocks.ndim - 2)
    core = position % 2
    sibling = [(i, i ^ 1) for i in range(size)]

    def holds(partner):
        return (((sources ^ partner) & ~mask) == 0).reshape(shape)

    mine = jnp.where(core == 0, blocks[:, 0], blocks[:, 1])
    theirs = jnp.where(core == 0, blocks[:, 1], blocks[:, 0])
    received = lax.ppermute(theirs, axis, sibling)
    carried = jnp.where(holds(position ^ 1), received, mine)
    mask = mask | 1
    levels = list(range(1, size.bit_length() - 1))
    for level in levels:
        step = 1 << level
        if mask & step:
            continue
        received = lax.ppermute(carried, axis, [(i, i ^ step) for i in range(size)])
        carried = jnp.where(holds(position ^ step), received, carried)
        mask = mask | step
    other = lax.ppermute(carried, axis, sibling)
    first = jnp.where(core == 0, carried, other)
    second = jnp.where(core == 0, other, carried)
    return jnp.stack([first, second], axis=1)


def partner_2(array, axis, distance):
    return lax.ppermute(array, axis, [(i, i ^ 1 << distance) for i in range(lax.axis_size(axis))])


def passed_along(array, axis, by):
    size = lax.axis_size(axis)
    pairs = [(i, i + by) for i in range(size) if 0 <= i + by < size]
    return lax.ppermute(array, axis, pairs)


LANES = 128


def attend_kernel(meta_ref, q_ref, g_ref, win_ref, glob_ref, *rest):
    partner_refs = rest[:RAND]
    att_ref, gq_ref, gwin_ref, gpart_ref, stats_ref = rest[RAND:]
    block_count = q_ref.shape[0] // BLOCK
    listed = 3 + GLOBALS + RAND
    scale_factor = HEAD_DIM ** (-0.5)
    gwin_ref[...] = jnp.zeros_like(gwin_ref)
    gpart_ref[...] = jnp.zeros_like(gpart_ref)
    lane = lax.broadcasted_iota(jnp.int32, (BLOCK, LANES), 1)
    per_pair = LANES // HEAD_DIM
    col = lax.broadcasted_iota(jnp.int32, (per_pair * BLOCK, listed * BLOCK), 1)
    nt = (((1,), (1,)), ((), ()))
    tn = (((0,), (0,)), ((), ()))
    base = (3 + GLOBALS) * BLOCK
    for j in range(block_count):
        rows = pl.ds(j * BLOCK, BLOCK)
        q = q_ref[rows, :]
        g = g_ref[rows, :]
        picks = [pl.multiple_of(meta_ref[j * RAND + r] * BLOCK, BLOCK) for r in range(RAND)]
        left_ok = meta_ref[block_count * RAND + j]
        right_ok = meta_ref[block_count * RAND + block_count + j]

        def gather(kv):
            parts = [win_ref[kv, pl.ds(j * BLOCK, 3 * BLOCK), :], glob_ref[kv]]
            for r in range(RAND):
                parts.append(partner_refs[r][kv, pl.ds(picks[r], BLOCK), :])
            return jnp.concatenate(parts, axis=0)

        k = gather(0)
        v = gather(1)
        invalid = ((col < BLOCK) & (left_ok == 0)) | (
            (col >= 2 * BLOCK) & (col < 3 * BLOCK) & (right_ok == 0)
        )
        heads = [(lane >= h * HEAD_DIM) & (lane < (h + 1) * HEAD_DIM) for h in range(per_pair)]
        qm = jnp.concatenate([jnp.where(m, q, jnp.zeros_like(q)) for m in heads], axis=0)
        gm = jnp.concatenate([jnp.where(m, g, jnp.zeros_like(g)) for m in heads], axis=0)
        scores = lax.dot_general(qm, k, nt, preferred_element_type=jnp.float32) * scale_factor
        scores = jnp.where(invalid, SCORE_FLOOR, scores)
        highest = jnp.max(scores, axis=-1, keepdims=True)
        raw_weights = jnp.exp(scores - highest)
        weight_total = jnp.sum(raw_weights, axis=-1, keepdims=True)
        probs = raw_weights / weight_total
        probs_low = probs.astype(jnp.bfloat16)
        grad_probs = lax.dot_general(gm, v, nt, preferred_element_type=jnp.float32)
        inner = jnp.sum(probs * grad_probs, axis=-1, keepdims=True)
        grad_scores = (scale_factor * probs * (grad_probs - inner)).astype(jnp.bfloat16)
        att_all = jnp.dot(probs_low, v, preferred_element_type=jnp.float32)
        gq_all = jnp.dot(grad_scores, k, preferred_element_type=jnp.float32)
        att = att_all[:BLOCK]
        gq = gq_all[:BLOCK]
        for h in range(1, per_pair):
            att = jnp.where(heads[h], att_all[h * BLOCK : (h + 1) * BLOCK], att)
            gq = jnp.where(heads[h], gq_all[h * BLOCK : (h + 1) * BLOCK], gq)
        gk = lax.dot_general(grad_scores, qm, tn, preferred_element_type=jnp.float32)
        gv = lax.dot_general(probs_low, gm, tn, preferred_element_type=jnp.float32)
        stacked_rows = per_pair * BLOCK
        for t, stat in enumerate((highest, weight_total, inner)):
            spread_out = jnp.transpose(jnp.broadcast_to(stat, (stacked_rows, stacked_rows)))
            stats_ref[0, pl.ds(j * 3 + t, 1), :] = spread_out[:1]
        att_ref[rows, :] = att.astype(att_ref.dtype)
        gq_ref[rows, :] = gq.astype(gq_ref.dtype)
        window = pl.ds(j * BLOCK, 3 * BLOCK)
        gwin_ref[0, window, :] += gk[: 3 * BLOCK]
        gwin_ref[1, window, :] += gv[: 3 * BLOCK]
        for r in range(RAND):
            there = pl.ds(picks[r], BLOCK)
            gpart_ref[r, 0, there, :] += gk[base + r * BLOCK : base + (r + 1) * BLOCK]
            gpart_ref[r, 1, there, :] += gv[base + r * BLOCK : base + (r + 1) * BLOCK]


def attend(meta, queries, grad_out, padded, glob, partners):
    tok_rows, width = queries.shape
    framed = padded.shape[1]
    pairs = width // LANES
    stat_rows = 3 * (tok_rows // BLOCK)
    row_spec = pl.BlockSpec((tok_rows, LANES), lambda p, m: (0, p))
    win_spec = pl.BlockSpec((2, framed, LANES), lambda p, m: (0, 0, p))
    glob_spec = pl.BlockSpec((2, glob.shape[1], LANES), lambda p, m: (0, 0, p))
    part_spec = pl.BlockSpec((2, tok_rows, LANES), lambda p, m: (0, 0, p))
    out_specs = [
        row_spec,
        row_spec,
        win_spec,
        pl.BlockSpec((RAND, 2, tok_rows, LANES), lambda p, m: (0, 0, 0, p)),
        pl.BlockSpec((1, stat_rows, LANES), lambda p, m: (p, 0, 0)),
    ]
    out_shape = [
        jax.ShapeDtypeStruct((tok_rows, width), jnp.bfloat16),
        jax.ShapeDtypeStruct((tok_rows, width), jnp.bfloat16),
        jax.ShapeDtypeStruct((2, framed, width), jnp.float32),
        jax.ShapeDtypeStruct((RAND, 2, tok_rows, width), jnp.float32),
        jax.ShapeDtypeStruct((pairs, stat_rows, LANES), jnp.float32),
    ]
    return pl.pallas_call(
        attend_kernel,
        grid_spec=pltpu.PrefetchScalarGridSpec(
            num_scalar_prefetch=1,
            grid=(pairs,),
            in_specs=[row_spec, row_spec, win_spec, glob_spec] + [part_spec] * RAND,
            out_specs=out_specs,
        ),
        out_shape=out_shape,
        compiler_params=pltpu.CompilerParams(dimension_semantics=("arbitrary",)),
    )(meta, queries, grad_out, padded, glob, *partners)


def partner_kernel(pick_ref, qd_ref, st_ref, kv_ref, out_ref):
    block_count = qd_ref.shape[1] // BLOCK
    per_pair = LANES // HEAD_DIM
    stacked_rows = per_pair * BLOCK
    scale_factor = HEAD_DIM ** (-0.5)
    nt = (((1,), (1,)), ((), ()))
    tn = (((0,), (0,)), ((), ()))
    out_ref[...] = jnp.zeros_like(out_ref)
    lane = lax.broadcasted_iota(jnp.int32, (BLOCK, LANES), 1)
    heads = [(lane >= h * HEAD_DIM) & (lane < (h + 1) * HEAD_DIM) for h in range(per_pair)]
    for j in range(block_count):
        rows = pl.ds(j * BLOCK, BLOCK)
        q = qd_ref[0, rows, :]
        g = qd_ref[1, rows, :]
        qm = jnp.concatenate([jnp.where(m, q, jnp.zeros_like(q)) for m in heads], axis=0)
        gm = jnp.concatenate([jnp.where(m, g, jnp.zeros_like(g)) for m in heads], axis=0)
        pick = pl.ds(pl.multiple_of(pick_ref[j] * BLOCK, BLOCK), BLOCK)
        k = kv_ref[0, pick, :]
        v = kv_ref[1, pick, :]
        highest, weight_total, inner = (
            jnp.transpose(
                jnp.broadcast_to(st_ref[0, pl.ds(j * 3 + t, 1), :], (stacked_rows, stacked_rows))
            )[:, :BLOCK]
            for t in range(3)
        )
        scores = lax.dot_general(qm, k, nt, preferred_element_type=jnp.float32) * scale_factor
        probs = jnp.exp(scores - highest) / weight_total
        probs_low = probs.astype(jnp.bfloat16)
        grad_probs = lax.dot_general(gm, v, nt, preferred_element_type=jnp.float32)
        grad_scores = (scale_factor * probs * (grad_probs - inner)).astype(jnp.bfloat16)
        out_ref[0, pick, :] += lax.dot_general(grad_scores, qm, tn, preferred_element_type=jnp.float32)
        out_ref[1, pick, :] += lax.dot_general(probs_low, gm, tn, preferred_element_type=jnp.float32)


def partner_terms(picks, qd, stats, stacked):
    _, tok_rows, width = stacked.shape
    pairs, stat_rows, _ = stats.shape
    slab_spec = pl.BlockSpec((2, tok_rows, LANES), lambda p, m: (0, 0, p))
    return pl.pallas_call(
        partner_kernel,
        grid_spec=pltpu.PrefetchScalarGridSpec(
            num_scalar_prefetch=1,
            grid=(pairs,),
            in_specs=[slab_spec, pl.BlockSpec((1, stat_rows, LANES), lambda p, m: (p, 0, 0)), slab_spec],
            out_specs=slab_spec,
        ),
        out_shape=jax.ShapeDtypeStruct((2, tok_rows, width), jnp.float32),
        compiler_params=pltpu.CompilerParams(dimension_semantics=("arbitrary",)),
    )(picks, qd, stats, stacked)


def local_body(queries, keys, values, grad_out, rand_blocks, global_ids):
    tok_rows, width = queries.shape
    block_count = tok_rows // BLOCK
    ctx_count = lax.axis_size("ctx")
    position = lax.axis_index("ctx")
    top_bit = ctx_count.bit_length() - 1
    block_iota = jnp.arange(block_count, dtype=jnp.int32)
    stacked = jnp.stack([keys, values])
    padded = padded_2(stacked, (("ctx", 1),), BLOCK)
    owners = global_ids // block_count
    local_ids = global_ids % block_count
    spread = [top_bit - 1 - matching for matching in range(RAND)]
    partners = []
    for bit in spread:
        partners.append(partner_2(stacked, "ctx", bit))
    far_qd = partner_2(jnp.stack([queries, grad_out]), "ctx", spread[0])
    far_picks = partner_2(rand_blocks[:, 0].astype(jnp.float32), "ctx", spread[0])
    candidates = [
        lax.dynamic_slice_in_dim(stacked, local_ids[global_slot] * BLOCK, BLOCK, 1)
        for global_slot in range(GLOBALS)
    ]
    fetched = from_root(jnp.stack(candidates), "ctx", owners, 0)
    glob = jnp.swapaxes(fetched, 0, 1).reshape(2, GLOBALS * BLOCK, width)
    global_block = position * block_count + block_iota
    seq_blocks = block_count * ctx_count
    meta = jnp.concatenate(
        [
            rand_blocks.reshape(-1).astype(jnp.int32),
            (global_block > 0).astype(jnp.int32),
            (global_block < seq_blocks - 1).astype(jnp.int32),
        ]
    )
    attended_out, grad_queries, gwin, gpart, stats = attend(
        meta, queries, grad_out, padded, glob, partners
    )
    low = jnp.bfloat16
    from_right = passed_along(gwin[:, :BLOCK].astype(low), "ctx", -1).astype(jnp.float32)
    from_left = passed_along(gwin[:, -BLOCK:].astype(low), "ctx", 1).astype(jnp.float32)
    own_total = gwin[:, BLOCK:-BLOCK]
    own_total = own_total.at[:, tok_rows - BLOCK :].add(from_right)
    own_total = own_total.at[:, :BLOCK].add(from_left)
    for matching in range(1, RAND):
        own_total = own_total + partner_2(gpart[matching].astype(low), "ctx", spread[matching]).astype(
            jnp.float32
        )
    far_stats = partner_2(stats, "ctx", spread[0])
    own_total = own_total + partner_terms(far_picks.astype(jnp.int32), far_qd, far_stats, stacked)
    grad_keys = own_total[0].astype(jnp.bfloat16)
    grad_values = own_total[1].astype(jnp.bfloat16)
    return (attended_out, grad_queries, grad_keys, grad_values)


def solution(mesh):
    placed = (
        P(("dp", "ctx"), None),
        P(("dp", "ctx"), None),
        P(("dp", "ctx"), None),
        P(("dp", "ctx"), None),
        P(("dp", "ctx"), None),
        P("dp"),
    )
    return jax.shard_map(
        local_body,
        mesh=mesh,
        in_specs=placed,
        out_specs=(
            P(("dp", "ctx"), None),
            P(("dp", "ctx"), None),
            P(("dp", "ctx"), None),
            P(("dp", "ctx"), None),
        ),
        check_vma=False,
    )
```
